32 devices in a mesh: tile: 8 (over z, x), chan: 4 (over y, core).
Axes of the slice: x: 2, y: 2, z: 4, core: 2. Of those that a mesh axis runs over, the one named last changes fastest.
Arguments:
- visibility: bfloat16 [128, 2, 8, 512], P('tile', None, 'chan'), may hold values from -6 to 6
- imaging_weight: bfloat16 [128, 8, 512], P('tile', 'chan'), may hold values from 0.19921875 to 5
- position: int32 [128, 2, 512], P('tile'), may hold values from 0 to 3615
- anchor: int32 [128, 2], P('tile'), may hold values from 0 to 128
- destination: int32 [128], P('tile'), may hold values from 0 to 7, as said below
- block_count: int32 [8], P('tile'), may hold values from 12 to 16, as said below
- kernel: float32 [32, 16], replicated, may hold values from 0.25 to 1.5
Outputs:
- combined_grid: float32 [2, 2048, 256], P(None, ('tile', 'chan'))
- residual: bfloat16 [128, 2, 8, 512], P('tile', None, 'chan')
The draws below stay inside these ranges and needn't reach their ends.
Inputs may be any that keep to these rules, and one draw needn't show every extreme that they name: `destination`: among each owner's 16 blocks at most 4 name one tile; one tile is named by exactly 4 blocks of every owner, all of them among that owner's first 8 blocks. Owner i's live blocks are its first block_count[i]; some owner has all 16 live. `position`: every entry is below 2^12. A program may carry positions, corners and other integer fields packed into fewer bits when they are sent, as long as nothing is lost.
All inputs are finite; a program needn't handle non-finite values.
Results may differ from the reference program's by a relative error of at most 0.009.
Values may be sent and summed in bfloat16 or wider, within the bound.
No kernel may reach another device: no remote copies, remote signals or barrier semaphores. Data moves between devices by JAX's collectives and lax.ppermute only.
A program may use at most 64 MiB of HBM per device.

```python
import math
import jax
import jax.numpy as jnp
import numpy as np
from jax import lax

BLOCK = 512
TAPS = 16
OS = 32
SUB = 128
TS = 256
BLK_DEV = 16
CAP = 4
BLOCKS = 128
CH = 8
N_TILE = 8


def draw_destination(key, part):
    base = jax.random.fold_in(key, 17)
    busy_key, favor_key, device_key = jax.random.split(base, 3)
    busiest = jax.random.randint(busy_key, (), 0, N_TILE)
    favored = (jax.random.randint(favor_key, (N_TILE,), 0, 4) == 0).astype(jnp.int32)
    pool_size = (N_TILE - 1) * CAP
    slot_ids = jnp.arange(pool_size, dtype=jnp.int32)
    pool_tile = slot_ids // CAP
    pool_tile = jnp.where(pool_tile >= busiest, pool_tile + 1, pool_tile)

    def one_device(dev_key):
        score_key, front_key, back_key = jax.random.split(dev_key, 3)
        levels = jax.random.randint(score_key, (pool_size,), 0, 1 << 16)
        scores = levels // (1 + 3 * favored[pool_tile]) * pool_size + slot_ids
        picked = pool_tile[jnp.argsort(scores)[:BLK_DEV - CAP]]
        rows_all = jnp.concatenate([jnp.full((CAP,), busiest, jnp.int32), picked.astype(jnp.int32)])
        front = jax.random.permutation(front_key, BLK_DEV // 2)
        behind = jax.random.permutation(back_key, BLK_DEV - BLK_DEV // 2) + BLK_DEV // 2
        placing = jnp.concatenate([front, behind])
        return rows_all[placing]
    every = jax.vmap(one_device)(jax.random.split(device_key, N_TILE))
    return every.reshape(N_TILE * BLK_DEV).astype(jnp.int32)


def draw_block_count(key, part):
    first_key, second_key = jax.random.split(jax.random.fold_in(key, 5))
    counts = jax.random.randint(first_key, (N_TILE,), BLK_DEV * 3 // 4, BLK_DEV + 1)
    fullest = jax.random.randint(second_key, (), 0, N_TILE)
    return jnp.where(jnp.arange(N_TILE) == fullest, BLK_DEV, counts).astype(jnp.int32)


def touch_ends(array, stream_key, smallest, high):
    spot = [jax.random.randint(jax.random.fold_in(stream_key, axis), (), 0, length) for axis, length in enumerate(array.shape)]
    longest = array.shape.index(max(array.shape))
    beside = spot[:longest] + [(spot[longest] + 1) % array.shape[longest]] + spot[longest + 1:]
    return array.at[tuple(spot)].set(smallest).at[tuple(beside)].set(high)


def block_levels(stream_key, shape, cuts, smallest, largest):
    gain, own = 1.0, jax.random.fold_in(stream_key, 6)
    for dim, parts in cuts:
        steps = jnp.exp(jax.random.uniform(jax.random.fold_in(own, dim), (parts,), jnp.float32, smallest / len(cuts), largest / len(cuts)))
        gain = gain * jnp.repeat(steps, shape[dim] // parts).reshape([-1 if axis == dim else 1 for axis in range(len(shape))])
    return gain


def normal_values(stream_key, shape, deviation, bound, cuts=(), kind=jnp.bfloat16):
    gain = block_levels(stream_key, shape, cuts, -0.22, 0.18) if cuts else 1.0
    array = jax.random.normal(stream_key, shape, jnp.float32) * deviation * gain
    return jnp.minimum(jnp.maximum(array, -bound), bound).astype(kind)


def setup_inputs(seed: int = 0) -> dict:
    streams_of = jax.random.split(jax.random.key(seed), 8)
    visibility = normal_values(streams_of[0], (BLOCKS, 2, CH, BLOCK), 1.0, 6.0, ((0, 8), (2, 4)))
    imaging_weight = jnp.clip(jnp.exp(math.log(5.0) - 3.2227897 * jax.random.uniform(streams_of[1], (BLOCKS, CH, BLOCK), jnp.float32) ** block_levels(streams_of[1], (BLOCKS, CH, BLOCK), ((0, 8), (1, 4)), -0.2, 0.2)), 0.19921875, 5.0).astype(jnp.bfloat16)
    position = touch_ends(jax.random.randint(streams_of[2], (BLOCKS, 2, BLOCK), 0, (SUB - TAPS + 1) * OS), jax.random.fold_in(streams_of[2], 1), 0, ((SUB - TAPS + 1) * OS) - 1).astype(jnp.int32)
    anchor = touch_ends(jax.random.randint(streams_of[3], (BLOCKS, 2), 0, TS - SUB + 1), jax.random.fold_in(streams_of[3], 1), 0, TS - SUB).astype(jnp.int32)
    destination = draw_destination(jax.random.fold_in(streams_of[7], 71), 0)
    block_count = draw_block_count(jax.random.fold_in(streams_of[7], 71), 0)
    kernel = jnp.clip(jax.random.uniform(streams_of[6], (OS, TAPS), jnp.float32, 0.25, 1.5), 0.25, 1.5)
    return {"visibility": visibility, "imaging_weight": imaging_weight, "position": position, "anchor": anchor, "destination": destination, "block_count": block_count, "kernel": kernel}


def tap_matrix(positions, kernel):
    cell_row = positions // OS
    offset = positions % OS
    tap_values = kernel[offset]
    cell_ids = jnp.arange(SUB, dtype=jnp.int32)
    distance = cell_ids[:, None] - cell_row[None, :]
    matrix = jnp.zeros((SUB, positions.shape[0]), jnp.float32)
    for tap_index in range(TAPS):
        matrix = matrix + jnp.where(distance == tap_index, tap_values[:, tap_index][None, :], jnp.float32(0.0))
    return matrix.astype(jnp.bfloat16)


def reference(visibility, imaging_weight, position, anchor, destination, block_count, kernel):
    channels = visibility.shape[2]
    block_ids = jnp.arange(visibility.shape[0], dtype=jnp.int32)
    is_live = (block_ids % BLK_DEV) < block_count[block_ids // BLK_DEV]
    anchor_zero = jnp.zeros((), jnp.int32)

    def grid_one(tile_grid, block_item):
        values, weights, positions, corner, target, alive = block_item
        row_taps = tap_matrix(positions[0], kernel)
        col_taps = tap_matrix(positions[1], kernel)
        scaled = values.astype(jnp.float32) * weights.astype(jnp.float32)[None]
        weighted = (scaled[..., None] * col_taps.T.astype(jnp.float32)[None, None]).astype(jnp.bfloat16)
        patches = jnp.einsum('iv,rcvj->rcij', row_taps.astype(jnp.float32), weighted.astype(jnp.float32))
        patches = jnp.where(alive, patches, jnp.float32(0.0))
        start_at = (target.astype(jnp.int32), anchor_zero, anchor_zero, corner[0].astype(jnp.int32), corner[1].astype(jnp.int32))
        current = lax.dynamic_slice(tile_grid, start_at, (1, 2, channels, SUB, SUB))
        tile_grid = lax.dynamic_update_slice(tile_grid, current + patches[None], start_at)
        return tile_grid, None

    tile_grid = jnp.zeros((N_TILE, 2, channels, TS, TS), jnp.float32)
    tile_grid, _ = lax.scan(grid_one, tile_grid, (visibility, imaging_weight, position, anchor, destination, is_live))
    partner_ids = np.arange(N_TILE) ^ (N_TILE // 2)
    flipped = tile_grid[partner_ids][..., ::-1, ::-1]
    symmetric = jnp.concatenate([tile_grid[:, 0:1] + flipped[:, 0:1], tile_grid[:, 1:2] - flipped[:, 1:2]], axis=1)
    combined_grid = jnp.sum(symmetric, axis=2).transpose(1, 0, 2, 3).reshape(2, N_TILE * TS, TS)

    def degrid_one(block_item):
        positions, corner, target, alive = block_item
        row_taps = tap_matrix(positions[0], kernel)
        col_taps = tap_matrix(positions[1], kernel)
        start_at = (target.astype(jnp.int32), anchor_zero, anchor_zero, corner[0].astype(jnp.int32), corner[1].astype(jnp.int32))
        window = lax.dynamic_slice(symmetric, start_at, (1, 2, channels, SUB, SUB))[0].astype(jnp.bfloat16)
        product = jnp.einsum('iv,rcij->rcvj', row_taps.astype(jnp.float32), window.astype(jnp.float32))
        predicted = jnp.sum(product * col_taps.T.astype(jnp.float32)[None, None], axis=-1) / (TAPS * TAPS)
        return jnp.where(alive, predicted, jnp.float32(0.0)).astype(jnp.bfloat16)

    predicted = lax.map(degrid_one, (position, anchor, destination, is_live))
    residual = (visibility.astype(jnp.float32) - predicted.astype(jnp.float32)).astype(jnp.bfloat16)
    return combined_grid, residual
```

```python
import functools

import jax
import jax.numpy as jnp
from jax import lax
from jax.experimental import pallas as pl
from jax.experimental.pallas import tpu as pltpu
from jax.sharding import PartitionSpec as P

TAPS = 16
OS = 32
SUB = 128
TS = 256
GROUP = 16


def from_partner(block, axis, apart):
    count = lax.axis_size(axis)
    route = []
    for low in range(count):
        high = low | 1 << apart
        if high != low and high < count:
            route += [(low, high), (high, low)]
    return lax.ppermute(block, axis, route)


def build_taps(tv_ref, base_ref, out_ref, item, axis, flip):
    width = out_ref.shape[1]
    base = base_ref[item, pl.ds(axis, 1), :]
    tv = tv_ref[item, axis].astype(jnp.float32)
    low_bits = base & (GROUP - 1)
    group_of = base >> 4
    rows = lax.broadcasted_iota(jnp.int32, (GROUP, width), 0)
    rows = jnp.where(flip, GROUP - 1 - rows, rows)
    reach = rows - low_bits
    wrapped = reach & (GROUP - 1)
    spread = jnp.zeros((GROUP, width), jnp.float32)
    for tap in range(TAPS):
        spread = jnp.where(wrapped == tap, tv[tap : tap + 1, :], spread)
    lower = jnp.where(reach >= 0, spread, 0.0)
    upper = jnp.where(reach < 0, spread, 0.0)
    lower_group = jnp.where(flip, GROUP - 1 - group_of, group_of)
    upper_group = jnp.where(flip, GROUP - 2 - group_of, group_of + 1)
    for part in range(TS // GROUP):
        piece = jnp.where(lower_group == part, lower, jnp.where(upper_group == part, upper, 0.0))
        out_ref[pl.ds(part * GROUP, GROUP), :] = piece


def grid_kernel(flags_ref, tv_ref, base_ref, scaled_ref, out_ref, row_ref, col_ref):
    items = tv_ref.shape[0]
    channels = scaled_ref.shape[2]
    out_ref[...] = jnp.zeros(out_ref.shape, jnp.float32)

    def body(item, carry):
        @pl.when(flags_ref[0, item] != 0)
        def _():
            flip = flags_ref[1, item] != 0
            build_taps(tv_ref, base_ref, row_ref, item, 0, flip)
            build_taps(tv_ref, base_ref, col_ref, item, 1, flip)
            row_taps = row_ref[...].astype(jnp.bfloat16)
            col_taps = col_ref[...]
            for part in range(2):
                for chan in range(channels):
                    scale = scaled_ref[item, part, pl.ds(chan, 1), :]
                    weighted = (scale * col_taps).astype(jnp.bfloat16)
                    out_ref[part, chan] += lax.dot_general(
                        row_taps,
                        weighted,
                        (((1,), (1,)), ((), ())),
                        preferred_element_type=jnp.float32,
                    )

        return carry

    lax.fori_loop(0, items, body, 0)


def degrid_kernel(flags_ref, tv_ref, base_ref, sym_ref, out_ref, row_ref, col_ref):
    items = tv_ref.shape[0]
    channels = sym_ref.shape[1]
    out_ref[...] = jnp.zeros(out_ref.shape, jnp.float32)

    def body(item, carry):
        @pl.when(flags_ref[0, item] != 0)
        def _():
            flip = flags_ref[1, item] != 0
            build_taps(tv_ref, base_ref, row_ref, item, 0, flip)
            build_taps(tv_ref, base_ref, col_ref, item, 1, flip)
            col_taps = col_ref[...].astype(jnp.bfloat16)
            row_taps = row_ref[...]
            norm = 1.0 / (TAPS * TAPS)
            for part in range(2):
                factor = jnp.where(flip, -norm, norm) if part == 1 else norm
                for chan in range(channels):
                    inner = jnp.dot(sym_ref[part, chan], col_taps, preferred_element_type=jnp.float32)
                    total = jnp.sum(row_taps * inner, axis=0, keepdims=True)
                    out_ref[item, part, pl.ds(chan, 1), :] = total * factor

        return carry

    lax.fori_loop(0, items, body, 0)


def run_grid(flags, tv, base, scaled):
    channels = scaled.shape[2]
    width = scaled.shape[3]
    vmem = pltpu.VMEM
    return pl.pallas_call(
        grid_kernel,
        out_shape=jax.ShapeDtypeStruct((2, channels, TS, TS), jnp.float32),
        in_specs=[
            pl.BlockSpec(memory_space=pltpu.SMEM),
            pl.BlockSpec(memory_space=vmem),
            pl.BlockSpec(memory_space=vmem),
            pl.BlockSpec(memory_space=vmem),
        ],
        out_specs=pl.BlockSpec(memory_space=vmem),
        scratch_shapes=[vmem((TS, width), jnp.float32), vmem((TS, width), jnp.float32)],
    )(flags, tv, base, scaled)


def run_degrid(flags, tv, base, sym):
    items = tv.shape[0]
    channels = sym.shape[1]
    width = tv.shape[3]
    vmem = pltpu.VMEM
    return pl.pallas_call(
        degrid_kernel,
        out_shape=jax.ShapeDtypeStruct((items, 2, channels, width), jnp.float32),
        in_specs=[
            pl.BlockSpec(memory_space=pltpu.SMEM),
            pl.BlockSpec(memory_space=vmem),
            pl.BlockSpec(memory_space=vmem),
            pl.BlockSpec(memory_space=vmem),
        ],
        out_specs=pl.BlockSpec(memory_space=vmem),
        scratch_shapes=[vmem((TS, width), jnp.float32), vmem((TS, width), jnp.float32)],
    )(flags, tv, base, sym)


def tap_values(positions, kernel):
    offset = positions % OS
    chosen = (offset[:, :, None, :] == jnp.arange(OS, dtype=jnp.int32)[None, None, :, None]).astype(
        jnp.float32
    )
    values = jnp.einsum("naov,ok->nakv", chosen, kernel, precision=lax.Precision.HIGHEST)
    return values.astype(jnp.bfloat16)


def per_device(visibility, imaging_weight, position, anchor, destination, block_count, kernel):
    tile_count = lax.axis_size("tile")
    mirror_bit = tile_count.bit_length() - 2
    owned_blocks = visibility.shape[0]
    bucket = max(2, 2 * owned_blocks // tile_count)
    slot_total = tile_count * bucket
    own_index = lax.axis_index("tile")
    lower_half = own_index < tile_count // 2
    block_ids = jnp.arange(owned_blocks, dtype=jnp.int32)
    is_live = block_ids < block_count[0]
    same_tile = destination[:, None] == destination[None, :]
    earlier = block_ids[None, :] < block_ids[:, None]
    rank_in_tile = jnp.sum((same_tile & earlier).astype(jnp.int32), axis=1)
    slot_of = destination * bucket + rank_in_tile
    slot_ids = jnp.arange(slot_total, dtype=jnp.int32)
    matches = slot_of[None, :] == slot_ids[:, None]
    filled = jnp.any(matches, axis=1)
    source = jnp.sum(jnp.where(matches, block_ids[None, :], 0), axis=1)
    send_values = jnp.where(
        filled[:, None, None, None], visibility[source], jnp.zeros((), jnp.bfloat16)
    )
    send_weights = jnp.where(
        filled[:, None, None], imaging_weight[source], jnp.zeros((), jnp.bfloat16)
    )
    send_positions = jnp.where(filled[:, None, None], position[source], 0)
    send_corner = jnp.where(filled[:, None], anchor[source], 0)
    send_live = (filled & is_live[source]).astype(jnp.int32)
    got_values, got_weights = (
        lax.all_to_all(send_values, "tile", split_axis=0, concat_axis=0, tiled=True),
        lax.all_to_all(send_weights, "tile", split_axis=0, concat_axis=0, tiled=True),
    )
    got_positions, got_corner, got_live = (
        lax.all_to_all(send_positions, "tile", split_axis=0, concat_axis=0, tiled=True),
        lax.all_to_all(send_corner, "tile", split_axis=0, concat_axis=0, tiled=True),
        lax.all_to_all(send_live, "tile", split_axis=0, concat_axis=0, tiled=True),
    )
    other_values, other_weights = from_partner((got_values, got_weights), "tile", mirror_bit)
    other_positions, other_corner, other_live = from_partner(
        (got_positions, got_corner, got_live), "tile", mirror_bit
    )

    def joined(mine_part, their_part):
        return jnp.where(
            lower_half,
            jnp.concatenate([mine_part, their_part]),
            jnp.concatenate([their_part, mine_part]),
        )

    all_values = joined(got_values, other_values)
    all_weights = joined(got_weights, other_weights)
    all_positions = joined(got_positions, other_positions)
    all_corner = joined(got_corner, other_corner)
    all_live = joined(got_live, other_live)
    rank = jnp.cumsum(all_live) - all_live
    pair_total = jnp.sum(all_live)
    middle = (pair_total + 1) // 2
    taken = jnp.where(lower_half, rank < middle, rank >= middle)
    mine = (all_live > 0) & taken
    item_ids = jnp.arange(2 * slot_total, dtype=jnp.int32)
    mirrored = (item_ids >= slot_total) == lower_half
    flags = jnp.stack([mine, mirrored]).astype(jnp.int32)

    base = all_corner[:, :, None] + all_positions // OS
    tv = tap_values(all_positions, kernel)
    conj_sign = jnp.where(mirrored, -1.0, 1.0).astype(jnp.float32)
    part_sign = jnp.stack([jnp.ones_like(conj_sign), conj_sign], axis=1)
    scaled = (
        all_values.astype(jnp.float32)
        * all_weights.astype(jnp.float32)[:, None]
        * part_sign[:, :, None, None]
    )

    tile_grid = run_grid(flags, tv, base, scaled)
    partner_grid = from_partner(tile_grid, "tile", mirror_bit)
    sign = jnp.array([1.0, -1.0], jnp.float32).reshape(2, 1, 1, 1)
    symmetric = tile_grid + partner_grid[:, :, ::-1, ::-1] * sign

    predicted = run_degrid(flags, tv, base, symmetric.astype(jnp.bfloat16)).astype(jnp.bfloat16)
    own_start = jnp.where(lower_half, 0, slot_total).astype(jnp.int32)
    their_start = (slot_total - own_start).astype(jnp.int32)
    own_part = lax.dynamic_slice_in_dim(predicted, own_start, slot_total, 0)
    their_part = lax.dynamic_slice_in_dim(predicted, their_start, slot_total, 0)
    own_results = own_part + from_partner(their_part, "tile", mirror_bit)
    combined_grid = lax.psum_scatter(
        jnp.sum(symmetric, axis=1), "chan", scatter_dimension=1, tiled=True
    )
    returned_slots = lax.all_to_all(own_results, "tile", split_axis=0, concat_axis=0, tiled=True)
    returned = jnp.where(
        is_live[:, None, None, None], returned_slots[slot_of], jnp.zeros((), jnp.bfloat16)
    )
    residual = (visibility.astype(jnp.float32) - returned.astype(jnp.float32)).astype(jnp.bfloat16)
    return (combined_grid, residual)


def solution(mesh):
    placed = (
        P("tile", None, "chan", None),
        P("tile", "chan", None),
        P("tile", None, None),
        P("tile", None),
        P("tile"),
        P("tile"),
        P(),
    )
    return jax.shard_map(
        per_device,
        mesh=mesh,
        in_specs=placed,
        out_specs=(P(None, ("tile", "chan"), None), P("tile", None, "chan", None)),
        check_vma=False,
    )
```

```python
import functools

import jax
import jax.numpy as jnp
from jax import lax
from jax.experimental import pallas as pl
from jax.experimental.pallas import tpu as pltpu
from jax.sharding import PartitionSpec as P

TAPS = 16
OS = 32
SUB = 128
TS = 256
GROUP = 16


def from_partner(block, axis, apart):
    count = lax.axis_size(axis)
    route = []
    for low in range(count):
        high = low | 1 << apart
        if high != low and high < count:
            route += [(low, high), (high, low)]
    return lax.ppermute(block, axis, route)


def build_taps(tv_ref, base_ref, out_ref, item, axis, flip):
    width = out_ref.shape[1]
    base = base_ref[item, pl.ds(axis, 1), :]
    tv = tv_ref[item, axis].astype(jnp.float32)
    low_bits = base & (GROUP - 1)
    group_of = base >> 4
    rows = lax.broadcasted_iota(jnp.int32, (GROUP, width), 0)
    rows = jnp.where(flip, GROUP - 1 - rows, rows)
    reach = rows - low_bits
    wrapped = reach & (GROUP - 1)
    spread = jnp.zeros((GROUP, width), jnp.float32)
    for tap in range(TAPS):
        spread = jnp.where(wrapped == tap, tv[tap : tap + 1, :], spread)
    lower = jnp.where(reach >= 0, spread, 0.0)
    upper = jnp.where(reach < 0, spread, 0.0)
    lower_group = jnp.where(flip, GROUP - 1 - group_of, group_of)
    upper_group = jnp.where(flip, GROUP - 2 - group_of, group_of + 1)
    for part in range(TS // GROUP):
        piece = jnp.where(lower_group == part, lower, jnp.where(upper_group == part, upper, 0.0))
        out_ref[pl.ds(part * GROUP, GROUP), :] = piece


def grid_kernel(flags_ref, tv_ref, base_ref, scaled_ref, sum_ref, sym_ref, acc_ref, row_ref, col_ref):
    items = tv_ref.shape[0]
    channels = scaled_ref.shape[2]
    acc_ref[...] = jnp.zeros(acc_ref.shape, jnp.float32)

    def body(item, carry):
        @pl.when(flags_ref[0, item] != 0)
        def _():
            flip = flags_ref[1, item] != 0
            build_taps(tv_ref, base_ref, row_ref, item, 0, flip)
            build_taps(tv_ref, base_ref, col_ref, item, 1, flip)
            row_taps = row_ref[...].astype(jnp.bfloat16)
            col_taps = col_ref[...]
            for part in range(2):
                for chan in range(channels):
                    scale = scaled_ref[item, part, pl.ds(chan, 1), :]
                    weighted = (scale * col_taps).astype(jnp.bfloat16)
                    acc_ref[part, chan] += lax.dot_general(
                        row_taps,
                        weighted,
                        (((1,), (1,)), ((), ())),
                        preferred_element_type=jnp.float32,
                    )

        return carry

    lax.fori_loop(0, items, body, 0)
    for part in range(2):
        total = acc_ref[part, 0]
        sym_ref[part, 0] = total.astype(jnp.bfloat16)
        for chan in range(1, channels):
            layer = acc_ref[part, chan]
            sym_ref[part, chan] = layer.astype(jnp.bfloat16)
            total = total + layer
        sum_ref[part] = total


def degrid_kernel(flags_ref, tv_ref, base_ref, sym_ref, out_ref, row_ref, col_ref):
    items = tv_ref.shape[0]
    channels = sym_ref.shape[1]
    out_ref[...] = jnp.zeros(out_ref.shape, jnp.float32)

    def body(item, carry):
        @pl.when((flags_ref[0, item] != 0) & (flags_ref[1, item] == 0))
        def _():
            build_taps(tv_ref, base_ref, row_ref, item, 0, False)
            build_taps(tv_ref, base_ref, col_ref, item, 1, False)
            col_taps = col_ref[...].astype(jnp.bfloat16)
            row_taps = row_ref[...]
            norm = 1.0 / (TAPS * TAPS)
            for part in range(2):
                for chan in range(channels):
                    inner = jnp.dot(sym_ref[part, chan], col_taps, preferred_element_type=jnp.float32)
                    total = jnp.sum(row_taps * inner, axis=0, keepdims=True)
                    out_ref[item, part, pl.ds(chan, 1), :] = total * norm

        return carry

    lax.fori_loop(0, items, body, 0)


def run_grid(flags, tv, base, scaled):
    channels = scaled.shape[2]
    width = scaled.shape[3]
    vmem = pltpu.VMEM
    return pl.pallas_call(
        grid_kernel,
        out_shape=(
            jax.ShapeDtypeStruct((2, TS, TS), jnp.float32),
            jax.ShapeDtypeStruct((2, channels, TS, TS), jnp.bfloat16),
        ),
        in_specs=[
            pl.BlockSpec(memory_space=pltpu.SMEM),
            pl.BlockSpec(memory_space=vmem),
            pl.BlockSpec(memory_space=vmem),
            pl.BlockSpec(memory_space=vmem),
        ],
        out_specs=(pl.BlockSpec(memory_space=vmem), pl.BlockSpec(memory_space=vmem)),
        scratch_shapes=[
            vmem((2, channels, TS, TS), jnp.float32),
            vmem((TS, width), jnp.float32),
            vmem((TS, width), jnp.float32),
        ],
    )(flags, tv, base, scaled)


def run_degrid(flags, tv, base, sym):
    items = tv.shape[0]
    channels = sym.shape[1]
    width = tv.shape[3]
    vmem = pltpu.VMEM
    return pl.pallas_call(
        degrid_kernel,
        out_shape=jax.ShapeDtypeStruct((items, 2, channels, width), jnp.float32),
        in_specs=[
            pl.BlockSpec(memory_space=pltpu.SMEM),
            pl.BlockSpec(memory_space=vmem),
            pl.BlockSpec(memory_space=vmem),
            pl.BlockSpec(memory_space=vmem),
        ],
        out_specs=pl.BlockSpec(memory_space=vmem),
        scratch_shapes=[vmem((TS, width), jnp.float32), vmem((TS, width), jnp.float32)],
    )(flags, tv, base, sym)


def tap_values(offset, kernel):
    chosen = (offset[:, :, None, :] == jnp.arange(OS, dtype=jnp.int32)[None, None, :, None]).astype(
        jnp.float32
    )
    values = jnp.einsum("naov,ok->nakv", chosen, kernel, precision=lax.Precision.HIGHEST)
    return values.astype(jnp.bfloat16)


def per_device(visibility, imaging_weight, position, anchor, destination, block_count, kernel):
    tile_count = lax.axis_size("tile")
    mirror_bit = tile_count.bit_length() - 2
    owned_blocks, _, channels, block_width = visibility.shape
    bucket = max(2, 2 * owned_blocks // tile_count)
    slot_total = tile_count * bucket
    group = 2 * bucket
    block_ids = jnp.arange(owned_blocks, dtype=jnp.int32)
    is_live = block_ids < block_count[0]
    same_tile = destination[:, None] == destination[None, :]
    earlier = block_ids[None, :] < block_ids[:, None]
    rank_in_tile = jnp.sum((same_tile & earlier).astype(jnp.int32), axis=1)
    slot_of = destination * bucket + rank_in_tile
    partner_of = destination ^ (1 << mirror_bit)
    first_slot = destination * group + rank_in_tile
    second_slot = partner_of * group + bucket + rank_in_tile

    base = anchor[:, :, None] + position // OS
    offset = position % OS
    live_row = jnp.broadcast_to(is_live[:, None, None], (owned_blocks, 1, block_width))
    packed = jnp.concatenate(
        [
            visibility.reshape(owned_blocks, 2 * channels, block_width),
            imaging_weight,
            base.astype(jnp.bfloat16),
            offset.astype(jnp.bfloat16),
            live_row.astype(jnp.bfloat16),
        ],
        axis=1,
    )
    slot_ids = jnp.arange(tile_count * group, dtype=jnp.int32)
    matches = (first_slot[None, :] == slot_ids[:, None]) | (second_slot[None, :] == slot_ids[:, None])
    filled = jnp.any(matches, axis=1)
    source = jnp.sum(jnp.where(matches, block_ids[None, :], 0), axis=1)
    send = jnp.where(filled[:, None, None], packed[source], jnp.zeros((), jnp.bfloat16))
    got = lax.all_to_all(send, "tile", split_axis=0, concat_axis=0, tiled=True)

    items = tile_count * group
    got_values = got[:, : 2 * channels].reshape(items, 2, channels, block_width)
    got_weights = got[:, 2 * channels : 3 * channels]
    got_base = got[:, 3 * channels : 3 * channels + 2].astype(jnp.int32)
    got_offset = got[:, 3 * channels + 2 : 3 * channels + 4].astype(jnp.int32)
    got_live = got[:, 3 * channels + 4, 0] > 0
    mirrored = (slot_ids % group) >= bucket
    flags = jnp.stack([got_live, mirrored]).astype(jnp.int32)

    tv = tap_values(got_offset, kernel)
    conj_sign = jnp.where(mirrored, -1.0, 1.0).astype(jnp.float32)
    part_sign = jnp.stack([jnp.ones_like(conj_sign), conj_sign], axis=1)
    scaled = (
        got_values.astype(jnp.float32)
        * got_weights.astype(jnp.float32)[:, None]
        * part_sign[:, :, None, None]
    )

    grid_sum, symmetric = run_grid(flags, tv, got_base, scaled)
    combined_grid = lax.psum_scatter(grid_sum, "chan", scatter_dimension=1, tiled=True)
    predicted = run_degrid(flags, tv, got_base, symmetric).astype(jnp.bfloat16)
    own_results = predicted.reshape(tile_count, group, 2, channels, block_width)[:, :bucket]
    own_results = own_results.reshape(slot_total, 2, channels, block_width)
    returned_slots = lax.all_to_all(own_results, "tile", split_axis=0, concat_axis=0, tiled=True)
    returned = jnp.where(
        is_live[:, None, None, None], returned_slots[slot_of], jnp.zeros((), jnp.bfloat16)
    )
    residual = (visibility.astype(jnp.float32) - returned.astype(jnp.float32)).astype(jnp.bfloat16)
    return (combined_grid, residual)


def solution(mesh):
    placed = (
        P("tile", None, "chan", None),
        P("tile", "chan", None),
        P("tile", None, None),
        P("tile", None),
        P("tile"),
        P("tile"),
        P(),
    )
    return jax.shard_map(
        per_device,
        mesh=mesh,
        in_specs=placed,
        out_specs=(P(None, ("tile", "chan"), None), P("tile", None, "chan", None)),
        check_vma=False,
    )
```

```python
import functools

import jax
import jax.numpy as jnp
from jax import lax
from jax.experimental import pallas as pl
from jax.experimental.pallas import tpu as pltpu
from jax.sharding import PartitionSpec as P

TAPS = 16
OS = 32
SUB = 128
TS = 256
GROUP = 16
WINDOW = SUB + GROUP


def from_partner(block, axis, apart):
    count = lax.axis_size(axis)
    route = []
    for low in range(count):
        high = low | 1 << apart
        if high != low and high < count:
            route += [(low, high), (high, low)]
    return lax.ppermute(block, axis, route)


def build_taps(tv_ref, base_ref, out_ref, item, axis, flip, origin):
    rows_out, width = out_ref.shape
    base = base_ref[item, pl.ds(axis, 1), :]
    base = jnp.where(flip, TS - TAPS - base, base) - origin
    tv = tv_ref[item, axis].astype(jnp.float32)
    low_bits = base & (GROUP - 1)
    group_of = base >> 4
    rows = lax.broadcasted_iota(jnp.int32, (GROUP, width), 0)
    reach = rows - low_bits
    wrapped = reach & (GROUP - 1)
    index = jnp.where(flip, TAPS - 1 - wrapped, wrapped)
    spread = jnp.zeros((GROUP, width), jnp.float32)
    for tap in range(TAPS):
        spread = jnp.where(index == tap, tv[tap : tap + 1, :], spread)
    lower = jnp.where(reach >= 0, spread, 0.0)
    upper = jnp.where(reach < 0, spread, 0.0)
    for part in range(rows_out // GROUP):
        piece = jnp.where(group_of == part, lower, jnp.where(group_of + 1 == part, upper, 0.0))
        out_ref[pl.ds(part * GROUP, GROUP), :] = piece


def grid_kernel(flags_ref, tv_ref, base_ref, scaled_ref, sum_ref, sym_ref, acc_ref, row_ref, col_ref):
    items = tv_ref.shape[0]
    channels = scaled_ref.shape[2]
    acc_ref[...] = jnp.zeros(acc_ref.shape, jnp.float32)

    def body(item, carry):
        @pl.when(flags_ref[0, item] != 0)
        def _():
            flip = flags_ref[1, item] != 0
            origin = pl.multiple_of(flags_ref[2, item], GROUP)
            build_taps(tv_ref, base_ref, row_ref, item, 0, flip, origin)
            build_taps(tv_ref, base_ref, col_ref, item, 1, flip, 0)
            window = row_ref.shape[0]
            row_taps = row_ref[...].astype(jnp.bfloat16)
            col_taps = col_ref[...]
            for part in range(2):
                for chan in range(channels):
                    scale = scaled_ref[item, part, pl.ds(chan, 1), :]
                    weighted = (scale * col_taps).astype(jnp.bfloat16)
                    acc_ref[part, chan, pl.ds(origin, window), :] += lax.dot_general(
                        row_taps,
                        weighted,
                        (((1,), (1,)), ((), ())),
                        preferred_element_type=jnp.float32,
                    )

        return carry

    lax.fori_loop(0, items, body, 0)
    for part in range(2):
        total = acc_ref[part, 0]
        sym_ref[part, 0] = total.astype(jnp.bfloat16)
        for chan in range(1, channels):
            layer = acc_ref[part, chan]
            sym_ref[part, chan] = layer.astype(jnp.bfloat16)
            total = total + layer
        sum_ref[part] = total


def degrid_kernel(flags_ref, tv_ref, base_ref, sym_ref, out_ref, row_ref, col_ref):
    items = tv_ref.shape[0]
    channels = sym_ref.shape[1]
    out_ref[...] = jnp.zeros(out_ref.shape, jnp.float32)

    def body(item, carry):
        @pl.when((flags_ref[0, item] != 0) & (flags_ref[1, item] == 0))
        def _():
            origin = pl.multiple_of(flags_ref[2, item], GROUP)
            build_taps(tv_ref, base_ref, row_ref, item, 0, False, origin)
            build_taps(tv_ref, base_ref, col_ref, item, 1, False, 0)
            window = row_ref.shape[0]
            col_taps = col_ref[...].astype(jnp.bfloat16)
            row_taps = row_ref[...]
            norm = 1.0 / (TAPS * TAPS)
            for part in range(2):
                for chan in range(channels):
                    inner = jnp.dot(sym_ref[part, chan, pl.ds(origin, window), :], col_taps, preferred_element_type=jnp.float32)
                    total = jnp.sum(row_taps * inner, axis=0, keepdims=True)
                    out_ref[item, part, pl.ds(chan, 1), :] = total * norm

        return carry

    lax.fori_loop(0, items, body, 0)


def run_grid(flags, tv, base, scaled):
    channels = scaled.shape[2]
    width = scaled.shape[3]
    vmem = pltpu.VMEM
    return pl.pallas_call(
        grid_kernel,
        out_shape=(
            jax.ShapeDtypeStruct((2, TS, TS), jnp.float32),
            jax.ShapeDtypeStruct((2, channels, TS, TS), jnp.bfloat16),
        ),
        in_specs=[
            pl.BlockSpec(memory_space=pltpu.SMEM),
            pl.BlockSpec(memory_space=vmem),
            pl.BlockSpec(memory_space=vmem),
            pl.BlockSpec(memory_space=vmem),
        ],
        out_specs=(pl.BlockSpec(memory_space=vmem), pl.BlockSpec(memory_space=vmem)),
        scratch_shapes=[
            vmem((2, channels, TS, TS), jnp.float32),
            vmem((WINDOW, width), jnp.float32),
            vmem((TS, width), jnp.float32),
        ],
    )(flags, tv, base, scaled)


def run_degrid(flags, tv, base, sym):
    items = tv.shape[0]
    channels = sym.shape[1]
    width = tv.shape[3]
    vmem = pltpu.VMEM
    return pl.pallas_call(
        degrid_kernel,
        out_shape=jax.ShapeDtypeStruct((items, 2, channels, width), jnp.float32),
        in_specs=[
            pl.BlockSpec(memory_space=pltpu.SMEM),
            pl.BlockSpec(memory_space=vmem),
            pl.BlockSpec(memory_space=vmem),
            pl.BlockSpec(memory_space=vmem),
        ],
        out_specs=pl.BlockSpec(memory_space=vmem),
        scratch_shapes=[vmem((WINDOW, width), jnp.float32), vmem((TS, width), jnp.float32)],
    )(flags, tv, base, sym)


def tap_values(offset, kernel):
    chosen = (offset[:, :, None, :] == jnp.arange(OS, dtype=jnp.int32)[None, None, :, None]).astype(
        jnp.float32
    )
    values = jnp.einsum("naov,ok->nakv", chosen, kernel, precision=lax.Precision.HIGHEST)
    return values.astype(jnp.bfloat16)


def per_device(visibility, imaging_weight, position, anchor, destination, block_count, kernel):
    tile_count = lax.axis_size("tile")
    mirror_bit = tile_count.bit_length() - 2
    owned_blocks, _, channels, block_width = visibility.shape
    bucket = max(2, 2 * owned_blocks // tile_count)
    slot_total = tile_count * bucket
    group = 2 * bucket
    block_ids = jnp.arange(owned_blocks, dtype=jnp.int32)
    is_live = block_ids < block_count[0]
    same_tile = destination[:, None] == destination[None, :]
    earlier = block_ids[None, :] < block_ids[:, None]
    rank_in_tile = jnp.sum((same_tile & earlier).astype(jnp.int32), axis=1)
    slot_of = destination * bucket + rank_in_tile
    partner_of = destination ^ (1 << mirror_bit)
    first_slot = destination * group + rank_in_tile
    second_slot = partner_of * group + bucket + rank_in_tile

    base = anchor[:, :, None] + position // OS
    offset = position % OS
    live_row = jnp.broadcast_to(is_live[:, None, None], (owned_blocks, 1, block_width))
    packed = jnp.concatenate(
        [
            visibility.reshape(owned_blocks, 2 * channels, block_width),
            imaging_weight,
            base.astype(jnp.bfloat16),
            offset.astype(jnp.bfloat16),
            live_row.astype(jnp.bfloat16),
        ],
        axis=1,
    )
    slot_ids = jnp.arange(tile_count * group, dtype=jnp.int32)
    matches = (first_slot[None, :] == slot_ids[:, None]) | (second_slot[None, :] == slot_ids[:, None])
    filled = jnp.any(matches, axis=1)
    source = jnp.sum(jnp.where(matches, block_ids[None, :], 0), axis=1)
    send = jnp.where(filled[:, None, None], packed[source], jnp.zeros((), jnp.bfloat16))
    got = lax.all_to_all(send, "tile", split_axis=0, concat_axis=0, tiled=True)

    items = tile_count * group
    got_values = got[:, : 2 * channels].reshape(items, 2, channels, block_width)
    got_weights = got[:, 2 * channels : 3 * channels]
    got_base = got[:, 3 * channels : 3 * channels + 2].astype(jnp.int32)
    got_offset = got[:, 3 * channels + 2 : 3 * channels + 4].astype(jnp.int32)
    got_live = got[:, 3 * channels + 4, 0] > 0
    mirrored = (slot_ids % group) >= bucket
    row_base = got_base[:, 0]
    lowest = jnp.where(mirrored, TS - TAPS - jnp.max(row_base, axis=1), jnp.min(row_base, axis=1))
    origin = jnp.minimum(lowest // GROUP * GROUP, TS - WINDOW)
    flags = jnp.stack([got_live.astype(jnp.int32), mirrored.astype(jnp.int32), origin])

    tv = tap_values(got_offset, kernel)
    conj_sign = jnp.where(mirrored, -1.0, 1.0).astype(jnp.float32)
    part_sign = jnp.stack([jnp.ones_like(conj_sign), conj_sign], axis=1)
    scaled = (
        got_values.astype(jnp.float32)
        * got_weights.astype(jnp.float32)[:, None]
        * part_sign[:, :, None, None]
    )

    grid_sum, symmetric = run_grid(flags, tv, got_base, scaled)
    combined_grid = lax.psum_scatter(grid_sum, "chan", scatter_dimension=1, tiled=True)
    predicted = run_degrid(flags, tv, got_base, symmetric).astype(jnp.bfloat16)
    own_results = predicted.reshape(tile_count, group, 2, channels, block_width)[:, :bucket]
    own_results = own_results.reshape(slot_total, 2, channels, block_width)
    returned_slots = lax.all_to_all(own_results, "tile", split_axis=0, concat_axis=0, tiled=True)
    returned = jnp.where(
        is_live[:, None, None, None], returned_slots[slot_of], jnp.zeros((), jnp.bfloat16)
    )
    residual = (visibility.astype(jnp.float32) - returned.astype(jnp.float32)).astype(jnp.bfloat16)
    return (combined_grid, residual)


def solution(mesh):
    placed = (
        P("tile", None, "chan", None),
        P("tile", "chan", None),
        P("tile", None, None),
        P("tile", None),
        P("tile"),
        P("tile"),
        P(),
    )
    return jax.shard_map(
        per_device,
        mesh=mesh,
        in_specs=placed,
        out_specs=(P(None, ("tile", "chan"), None), P("tile", None, "chan", None)),
        check_vma=False,
    )
```

```python
import functools

import jax
import jax.numpy as jnp
from jax import lax
from jax.experimental import pallas as pl
from jax.experimental.pallas import tpu as pltpu
from jax.sharding import PartitionSpec as P

TAPS = 16
OS = 32
SUB = 128
TS = 256
GROUP = 16
WINDOW = SUB + GROUP


def from_partner(block, axis, apart):
    count = lax.axis_size(axis)
    route = []
    for low in range(count):
        high = low | 1 << apart
        if high != low and high < count:
            route += [(low, high), (high, low)]
    return lax.ppermute(block, axis, route)


def build_taps(tv_ref, base_ref, out_ref, item, axis, flip, origin):
    rows_out, width = out_ref.shape
    base = base_ref[item, pl.ds(axis, 1), :]
    base = jnp.where(flip, TS - TAPS - base, base) - origin
    tv = tv_ref[item, axis].astype(jnp.float32)
    low_bits = base & (GROUP - 1)
    group_of = base >> 4
    rows = lax.broadcasted_iota(jnp.int32, (GROUP, width), 0)
    reach = rows - low_bits
    wrapped = reach & (GROUP - 1)
    index = jnp.where(flip, TAPS - 1 - wrapped, wrapped)
    spread = jnp.zeros((GROUP, width), jnp.float32)
    for tap in range(TAPS):
        spread = jnp.where(index == tap, tv[tap : tap + 1, :], spread)
    lower = jnp.where(reach >= 0, spread, 0.0)
    upper = jnp.where(reach < 0, spread, 0.0)
    for part in range(rows_out // GROUP):
        piece = jnp.where(group_of == part, lower, jnp.where(group_of + 1 == part, upper, 0.0))
        out_ref[pl.ds(part * GROUP, GROUP), :] = piece


def grid_kernel(final, flags_ref, tv_ref, base_ref, scaled_ref, acc_in_ref, *rest):
    if final:
        sum_ref, sym_ref, acc_ref, row_ref, col_ref = rest
    else:
        acc_ref, row_ref, col_ref = rest
    items = tv_ref.shape[0]
    channels = scaled_ref.shape[2]
    acc_ref[...] = acc_in_ref[...]

    def body(item, carry):
        @pl.when(flags_ref[0, item] != 0)
        def _():
            flip = flags_ref[1, item] != 0
            origin = pl.multiple_of(flags_ref[2, item], GROUP)
            build_taps(tv_ref, base_ref, row_ref, item, 0, flip, origin)
            build_taps(tv_ref, base_ref, col_ref, item, 1, flip, 0)
            window = row_ref.shape[0]
            row_taps = row_ref[...].astype(jnp.bfloat16)
            col_taps = col_ref[...]
            for part in range(2):
                for chan in range(channels):
                    scale = scaled_ref[item, part, pl.ds(chan, 1), :]
                    weighted = (scale * col_taps).astype(jnp.bfloat16)
                    acc_ref[part, chan, pl.ds(origin, window), :] += lax.dot_general(
                        row_taps,
                        weighted,
                        (((1,), (1,)), ((), ())),
                        preferred_element_type=jnp.float32,
                    )

        return carry

    lax.fori_loop(0, items, body, 0)
    if final:
        for part in range(2):
            total = acc_ref[part, 0]
            sym_ref[part, 0] = total.astype(jnp.bfloat16)
            for chan in range(1, channels):
                layer = acc_ref[part, chan]
                sym_ref[part, chan] = layer.astype(jnp.bfloat16)
                total = total + layer
            sum_ref[part] = total


def degrid_kernel(flags_ref, tv_ref, base_ref, sym_ref, out_ref, row_ref, col_ref):
    items = tv_ref.shape[0]
    channels = sym_ref.shape[1]
    out_ref[...] = jnp.zeros(out_ref.shape, jnp.float32)

    def body(item, carry):
        @pl.when((flags_ref[0, item] != 0) & (flags_ref[1, item] == 0))
        def _():
            origin = pl.multiple_of(flags_ref[2, item], GROUP)
            build_taps(tv_ref, base_ref, row_ref, item, 0, False, origin)
            build_taps(tv_ref, base_ref, col_ref, item, 1, False, 0)
            window = row_ref.shape[0]
            col_taps = col_ref[...].astype(jnp.bfloat16)
            row_taps = row_ref[...]
            norm = 1.0 / (TAPS * TAPS)
            for part in range(2):
                for chan in range(channels):
                    inner = jnp.dot(sym_ref[part, chan, pl.ds(origin, window), :], col_taps, preferred_element_type=jnp.float32)
                    total = jnp.sum(row_taps * inner, axis=0, keepdims=True)
                    out_ref[item, part, pl.ds(chan, 1), :] = total * norm

        return carry

    lax.fori_loop(0, items, body, 0)


def run_grid(flags, tv, base, scaled, acc_in, final):
    channels = scaled.shape[2]
    width = scaled.shape[3]
    vmem = pltpu.VMEM
    acc_shape = (2, channels, TS, TS)
    taps_scratch = [vmem((WINDOW, width), jnp.float32), vmem((TS, width), jnp.float32)]
    if final:
        out_shape = (
            jax.ShapeDtypeStruct((2, TS, TS), jnp.float32),
            jax.ShapeDtypeStruct(acc_shape, jnp.bfloat16),
        )
        out_specs = (pl.BlockSpec(memory_space=vmem), pl.BlockSpec(memory_space=vmem))
        scratch = [vmem(acc_shape, jnp.float32)] + taps_scratch
    else:
        out_shape = jax.ShapeDtypeStruct(acc_shape, jnp.float32)
        out_specs = pl.BlockSpec(memory_space=vmem)
        scratch = taps_scratch
    return pl.pallas_call(
        functools.partial(grid_kernel, final),
        out_shape=out_shape,
        in_specs=[pl.BlockSpec(memory_space=pltpu.SMEM)]
        + [pl.BlockSpec(memory_space=vmem) for _ in range(4)],
        out_specs=out_specs,
        scratch_shapes=scratch,
    )(flags, tv, base, scaled, acc_in)


def run_degrid(flags, tv, base, sym):
    items = tv.shape[0]
    channels = sym.shape[1]
    width = tv.shape[3]
    vmem = pltpu.VMEM
    return pl.pallas_call(
        degrid_kernel,
        out_shape=jax.ShapeDtypeStruct((items, 2, channels, width), jnp.float32),
        in_specs=[
            pl.BlockSpec(memory_space=pltpu.SMEM),
            pl.BlockSpec(memory_space=vmem),
            pl.BlockSpec(memory_space=vmem),
            pl.BlockSpec(memory_space=vmem),
        ],
        out_specs=pl.BlockSpec(memory_space=vmem),
        scratch_shapes=[vmem((WINDOW, width), jnp.float32), vmem((TS, width), jnp.float32)],
    )(flags, tv, base, sym)


def tap_values(offset, kernel):
    chosen = (offset[:, :, None, :] == jnp.arange(OS, dtype=jnp.int32)[None, None, :, None]).astype(
        jnp.float32
    )
    values = jnp.einsum("naov,ok->nakv", chosen, kernel, precision=lax.Precision.HIGHEST)
    return values.astype(jnp.bfloat16)


def unpack_slots(got, channels, mirrored, kernel):
    items, _, block_width = got.shape
    values = got[:, : 2 * channels].reshape(items, 2, channels, block_width)
    weights = got[:, 2 * channels : 3 * channels]
    base = got[:, 3 * channels : 3 * channels + 2].astype(jnp.int32)
    offset = got[:, 3 * channels + 2 : 3 * channels + 4].astype(jnp.int32)
    live = got[:, 3 * channels + 4, 0] > 0
    row_base = base[:, 0]
    if mirrored:
        lowest = TS - TAPS - jnp.max(row_base, axis=1)
    else:
        lowest = jnp.min(row_base, axis=1)
    origin = jnp.minimum(lowest // GROUP * GROUP, TS - WINDOW)
    flip = jnp.full((items,), int(mirrored), jnp.int32)
    flags = jnp.stack([live.astype(jnp.int32), flip, origin])
    tv = tap_values(offset, kernel)
    sign = jnp.array([1.0, -1.0 if mirrored else 1.0], jnp.float32).reshape(1, 2, 1, 1)
    scaled = values.astype(jnp.float32) * weights.astype(jnp.float32)[:, None] * sign
    return flags, tv, base, scaled


def per_device(visibility, imaging_weight, position, anchor, destination, block_count, kernel):
    tile_count = lax.axis_size("tile")
    mirror_bit = tile_count.bit_length() - 2
    owned_blocks, _, channels, block_width = visibility.shape
    bucket = max(2, 2 * owned_blocks // tile_count)
    slot_total = tile_count * bucket
    block_ids = jnp.arange(owned_blocks, dtype=jnp.int32)
    is_live = block_ids < block_count[0]
    same_tile = destination[:, None] == destination[None, :]
    earlier = block_ids[None, :] < block_ids[:, None]
    rank_in_tile = jnp.sum((same_tile & earlier).astype(jnp.int32), axis=1)
    slot_of = destination * bucket + rank_in_tile

    base = anchor[:, :, None] + position // OS
    offset = position % OS
    live_row = jnp.broadcast_to(is_live[:, None, None], (owned_blocks, 1, block_width))
    packed = jnp.concatenate(
        [
            visibility.reshape(owned_blocks, 2 * channels, block_width),
            imaging_weight,
            base.astype(jnp.bfloat16),
            offset.astype(jnp.bfloat16),
            live_row.astype(jnp.bfloat16),
        ],
        axis=1,
    )
    slot_ids = jnp.arange(slot_total, dtype=jnp.int32)

    def gather_slots(slots):
        matches = slots[None, :] == slot_ids[:, None]
        filled = jnp.any(matches, axis=1)
        source = jnp.sum(jnp.where(matches, block_ids[None, :], 0), axis=1)
        return jnp.where(filled[:, None, None], packed[source], jnp.zeros((), jnp.bfloat16))

    got_own = lax.all_to_all(gather_slots(slot_of), "tile", split_axis=0, concat_axis=0, tiled=True)
    got_other = from_partner(got_own, "tile", mirror_bit)

    own_flags, own_tv, own_base, own_scaled = unpack_slots(got_own, channels, False, kernel)
    zero_grid = jnp.zeros((2, channels, TS, TS), jnp.float32)
    partial_grid = run_grid(own_flags, own_tv, own_base, own_scaled, zero_grid, False)
    other_flags, other_tv, other_base, other_scaled = unpack_slots(got_other, channels, True, kernel)
    grid_sum, symmetric = run_grid(
        other_flags, other_tv, other_base, other_scaled, partial_grid, True
    )
    combined_grid = lax.psum_scatter(grid_sum, "chan", scatter_dimension=1, tiled=True)
    own_results = run_degrid(own_flags, own_tv, own_base, symmetric).astype(jnp.bfloat16)
    returned_slots = lax.all_to_all(own_results, "tile", split_axis=0, concat_axis=0, tiled=True)
    returned = jnp.where(
        is_live[:, None, None, None], returned_slots[slot_of], jnp.zeros((), jnp.bfloat16)
    )
    residual = (visibility.astype(jnp.float32) - returned.astype(jnp.float32)).astype(jnp.bfloat16)
    return (combined_grid, residual)


def solution(mesh):
    placed = (
        P("tile", None, "chan", None),
        P("tile", "chan", None),
        P("tile", None, None),
        P("tile", None),
        P("tile"),
        P("tile"),
        P(),
    )
    return jax.shard_map(
        per_device,
        mesh=mesh,
        in_specs=placed,
        out_specs=(P(None, ("tile", "chan"), None), P("tile", None, "chan", None)),
        check_vma=False,
    )
```

```python
import functools

import jax
import jax.numpy as jnp
from jax import lax
from jax.experimental import pallas as pl
from jax.experimental.pallas import tpu as pltpu
from jax.sharding import PartitionSpec as P

TAPS = 16
OS = 32
SUB = 128
TS = 256
GROUP = 16
WINDOW = SUB + GROUP


def from_partner(block, axis, apart):
    count = lax.axis_size(axis)
    route = []
    for low in range(count):
        high = low | 1 << apart
        if high != low and high < count:
            route += [(low, high), (high, low)]
    return lax.ppermute(block, axis, route)


def build_taps(tv, base, out_ref, flip, origin):
    rows_out, width = out_ref.shape
    if flip:
        base = TS - TAPS - base
    base = base - origin
    low_bits = base & (GROUP - 1)
    group_of = base >> 4
    rows = lax.broadcasted_iota(jnp.int32, (GROUP, width), 0)
    reach = rows - low_bits
    wrapped = reach & (GROUP - 1)
    index = TAPS - 1 - wrapped if flip else wrapped
    spread = jnp.zeros((GROUP, width), jnp.float32)
    for tap in range(TAPS):
        spread = jnp.where(index == tap, tv[tap : tap + 1, :], spread)
    lower = jnp.where(reach >= 0, spread, 0.0)
    upper = jnp.where(reach < 0, spread, 0.0)
    for part in range(rows_out // GROUP):
        piece = jnp.where(group_of == part, lower, jnp.where(group_of + 1 == part, upper, 0.0))
        out_ref[pl.ds(part * GROUP, GROUP), :] = piece


def item_fields(got_ref, table_ref, item, channels):
    fields = got_ref[item].astype(jnp.float32)
    width = fields.shape[1]
    lanes = lax.broadcasted_iota(jnp.int32, (OS, width), 0)
    table = table_ref[...]
    taps = []
    bases = []
    for axis in range(2):
        offset = fields[3 * channels + 2 + axis : 3 * channels + 3 + axis].astype(jnp.int32)
        chosen = (lanes == offset).astype(jnp.bfloat16)
        taps.append(jnp.dot(table, chosen, preferred_element_type=jnp.float32))
        bases.append(fields[3 * channels + axis : 3 * channels + 1 + axis].astype(jnp.int32))
    return fields, taps, bases


def grid_kernel(flip, first, flags_ref, table_ref, got_ref, *rest):
    if first:
        acc_ref, row_ref, col_ref = rest
        acc_ref[...] = jnp.zeros(acc_ref.shape, jnp.float32)
    else:
        acc_in_ref, sum_ref, sym_ref, acc_ref, row_ref, col_ref = rest
        acc_ref[...] = acc_in_ref[...]
    items = got_ref.shape[0]
    channels = acc_ref.shape[1]

    def body(item, carry):
        @pl.when(flags_ref[0, item] != 0)
        def _():
            origin = pl.multiple_of(flags_ref[1, item], GROUP)
            fields, taps, bases = item_fields(got_ref, table_ref, item, channels)
            build_taps(taps[0], bases[0], row_ref, flip, origin)
            build_taps(taps[1], bases[1], col_ref, flip, 0)
            window = row_ref.shape[0]
            row_taps = row_ref[...].astype(jnp.bfloat16)
            col_taps = col_ref[...]
            for part in range(2):
                for chan in range(channels):
                    row = part * channels + chan
                    scale = fields[row : row + 1] * fields[2 * channels + chan : 2 * channels + chan + 1]
                    if flip and part == 1:
                        scale = -scale
                    weighted = (scale * col_taps).astype(jnp.bfloat16)
                    acc_ref[part, chan, pl.ds(origin, window), :] += lax.dot_general(
                        row_taps,
                        weighted,
                        (((1,), (1,)), ((), ())),
                        preferred_element_type=jnp.float32,
                    )

        return carry

    lax.fori_loop(0, items, body, 0)
    if not first:
        for part in range(2):
            total = acc_ref[part, 0]
            sym_ref[part, 0] = total.astype(jnp.bfloat16)
            for chan in range(1, channels):
                layer = acc_ref[part, chan]
                sym_ref[part, chan] = layer.astype(jnp.bfloat16)
                total = total + layer
            sum_ref[part] = total


def degrid_kernel(flags_ref, table_ref, got_ref, sym_ref, out_ref, row_ref, col_ref):
    items = got_ref.shape[0]
    channels = sym_ref.shape[1]
    out_ref[...] = jnp.zeros(out_ref.shape, jnp.float32)

    def body(item, carry):
        @pl.when(flags_ref[0, item] != 0)
        def _():
            origin = pl.multiple_of(flags_ref[1, item], GROUP)
            _, taps, bases = item_fields(got_ref, table_ref, item, channels)
            build_taps(taps[0], bases[0], row_ref, False, origin)
            build_taps(taps[1], bases[1], col_ref, False, 0)
            window = row_ref.shape[0]
            col_taps = col_ref[...].astype(jnp.bfloat16)
            row_taps = row_ref[...]
            norm = 1.0 / (TAPS * TAPS)
            for part in range(2):
                for chan in range(channels):
                    inner = jnp.dot(
                        sym_ref[part, chan, pl.ds(origin, window), :],
                        col_taps,
                        preferred_element_type=jnp.float32,
                    )
                    total = jnp.sum(row_taps * inner, axis=0, keepdims=True)
                    out_ref[item, part, pl.ds(chan, 1), :] = total * norm

        return carry

    lax.fori_loop(0, items, body, 0)


def run_grid(flags, table, got, channels, flip, acc_in=None):
    width = got.shape[2]
    vmem = pltpu.VMEM
    acc_shape = (2, channels, TS, TS)
    taps_scratch = [vmem((WINDOW, width), jnp.float32), vmem((TS, width), jnp.float32)]
    first = acc_in is None
    if first:
        out_shape = jax.ShapeDtypeStruct(acc_shape, jnp.float32)
        out_specs = pl.BlockSpec(memory_space=vmem)
        scratch = taps_scratch
        operands = (flags, table, got)
    else:
        out_shape = (
            jax.ShapeDtypeStruct((2, TS, TS), jnp.float32),
            jax.ShapeDtypeStruct(acc_shape, jnp.bfloat16),
        )
        out_specs = (pl.BlockSpec(memory_space=vmem), pl.BlockSpec(memory_space=vmem))
        scratch = [vmem(acc_shape, jnp.float32)] + taps_scratch
        operands = (flags, table, got, acc_in)
    return pl.pallas_call(
        functools.partial(grid_kernel, flip, first),
        out_shape=out_shape,
        in_specs=[pl.BlockSpec(memory_space=pltpu.SMEM)]
        + [pl.BlockSpec(memory_space=vmem) for _ in operands[1:]],
        out_specs=out_specs,
        scratch_shapes=scratch,
    )(*operands)


def run_degrid(flags, table, got, sym):
    items, _, width = got.shape
    channels = sym.shape[1]
    vmem = pltpu.VMEM
    return pl.pallas_call(
        degrid_kernel,
        out_shape=jax.ShapeDtypeStruct((items, 2, channels, width), jnp.float32),
        in_specs=[pl.BlockSpec(memory_space=pltpu.SMEM)]
        + [pl.BlockSpec(memory_space=vmem) for _ in range(3)],
        out_specs=pl.BlockSpec(memory_space=vmem),
        scratch_shapes=[vmem((WINDOW, width), jnp.float32), vmem((TS, width), jnp.float32)],
    )(flags, table, got, sym)


def slot_flags(got, channels, mirrored):
    live = got[:, 3 * channels + 4, 0] > 0
    row_base = got[:, 3 * channels].astype(jnp.int32)
    if mirrored:
        lowest = TS - TAPS - jnp.max(row_base, axis=1)
    else:
        lowest = jnp.min(row_base, axis=1)
    origin = jnp.minimum(lowest // GROUP * GROUP, TS - WINDOW)
    return jnp.stack([live.astype(jnp.int32), origin])


def per_device(visibility, imaging_weight, position, anchor, destination, block_count, kernel):
    tile_count = lax.axis_size("tile")
    mirror_bit = tile_count.bit_length() - 2
    owned_blocks, _, channels, block_width = visibility.shape
    bucket = max(2, 2 * owned_blocks // tile_count)
    slot_total = tile_count * bucket
    block_ids = jnp.arange(owned_blocks, dtype=jnp.int32)
    is_live = block_ids < block_count[0]
    same_tile = destination[:, None] == destination[None, :]
    earlier = block_ids[None, :] < block_ids[:, None]
    rank_in_tile = jnp.sum((same_tile & earlier).astype(jnp.int32), axis=1)
    slot_of = destination * bucket + rank_in_tile

    base = anchor[:, :, None] + position // OS
    offset = position % OS
    live_row = jnp.broadcast_to(is_live[:, None, None], (owned_blocks, 1, block_width))
    packed = jnp.concatenate(
        [
            visibility.reshape(owned_blocks, 2 * channels, block_width),
            imaging_weight,
            base.astype(jnp.bfloat16),
            offset.astype(jnp.bfloat16),
            live_row.astype(jnp.bfloat16),
        ],
        axis=1,
    )
    slot_ids = jnp.arange(slot_total, dtype=jnp.int32)
    matches = slot_of[None, :] == slot_ids[:, None]
    filled = jnp.any(matches, axis=1)
    source = jnp.sum(jnp.where(matches, block_ids[None, :], 0), axis=1)
    send = jnp.where(filled[:, None, None], packed[source], jnp.zeros((), jnp.bfloat16))
    got_own = lax.all_to_all(send, "tile", split_axis=0, concat_axis=0, tiled=True)
    got_other = from_partner(got_own, "tile", mirror_bit)
    table = kernel.T.astype(jnp.bfloat16)

    own_flags = slot_flags(got_own, channels, False)
    partial_grid = run_grid(own_flags, table, got_own, channels, False)
    other_flags = slot_flags(got_other, channels, True)
    grid_sum, symmetric = run_grid(other_flags, table, got_other, channels, True, partial_grid)
    combined_grid = lax.psum_scatter(grid_sum, "chan", scatter_dimension=1, tiled=True)
    own_results = run_degrid(own_flags, table, got_own, symmetric).astype(jnp.bfloat16)
    returned_slots = lax.all_to_all(own_results, "tile", split_axis=0, concat_axis=0, tiled=True)
    returned = jnp.where(
        is_live[:, None, None, None], returned_slots[slot_of], jnp.zeros((), jnp.bfloat16)
    )
    residual = (visibility.astype(jnp.float32) - returned.astype(jnp.float32)).astype(jnp.bfloat16)
    return (combined_grid, residual)


def solution(mesh):
    placed = (
        P("tile", None, "chan", None),
        P("tile", "chan", None),
        P("tile", None, None),
        P("tile", None),
        P("tile"),
        P("tile"),
        P(),
    )
    return jax.shard_map(
        per_device,
        mesh=mesh,
        in_specs=placed,
        out_specs=(P(None, ("tile", "chan"), None), P("tile", None, "chan", None)),
        check_vma=False,
    )
```

```python
import functools

import jax
import jax.numpy as jnp
from jax import lax
from jax.experimental import pallas as pl
from jax.experimental.pallas import tpu as pltpu
from jax.sharding import PartitionSpec as P

TAPS = 16
OS = 32
SUB = 128
TS = 256
GROUP = 16
WINDOW = SUB + GROUP


def from_partner(block, axis, apart):
    count = lax.axis_size(axis)
    route = []
    for low in range(count):
        high = low | 1 << apart
        if high != low and high < count:
            route += [(low, high), (high, low)]
    return lax.ppermute(block, axis, route)


def build_taps(tv, base, out_ref, flip, origin):
    rows_out, width = out_ref.shape
    if flip:
        base = TS - TAPS - base
    base = base - origin
    low_bits = base & (GROUP - 1)
    group_of = base >> 4
    rows = lax.broadcasted_iota(jnp.int32, (GROUP, width), 0)
    reach = rows - low_bits
    wrapped = reach & (GROUP - 1)
    index = TAPS - 1 - wrapped if flip else wrapped
    spread = jnp.zeros((GROUP, width), jnp.float32)
    for tap in range(TAPS):
        spread = jnp.where(index == tap, tv[tap : tap + 1, :], spread)
    lower = jnp.where(reach >= 0, spread, 0.0)
    upper = jnp.where(reach < 0, spread, 0.0)
    for part in range(rows_out // GROUP):
        piece = jnp.where(group_of == part, lower, jnp.where(group_of + 1 == part, upper, 0.0))
        out_ref[pl.ds(part * GROUP, GROUP), :] = piece


def item_fields(got_ref, table_ref, item, channels):
    fields = got_ref[item].astype(jnp.float32)
    width = fields.shape[1]
    lanes = lax.broadcasted_iota(jnp.int32, (OS, width), 0)
    table = table_ref[...]
    taps = []
    bases = []
    for axis in range(2):
        offset = fields[3 * channels + 2 + axis : 3 * channels + 3 + axis].astype(jnp.int32)
        chosen = (lanes == offset).astype(jnp.bfloat16)
        taps.append(jnp.dot(table, chosen, preferred_element_type=jnp.float32))
        bases.append(fields[3 * channels + axis : 3 * channels + 1 + axis].astype(jnp.int32))
    return fields, taps, bases


def grid_kernel(flip, first, flags_ref, table_ref, got_ref, *rest):
    if first:
        acc_ref, row_ref, col_ref = rest
        acc_ref[...] = jnp.zeros(acc_ref.shape, jnp.float32)
    else:
        acc_in_ref, sum_ref, sym_ref, acc_ref, row_ref, col_ref = rest
        acc_ref[...] = acc_in_ref[...]
    items = got_ref.shape[0]
    channels = acc_ref.shape[1]

    def body(item, carry):
        @pl.when(flags_ref[0, item] != 0)
        def _():
            origin = pl.multiple_of(flags_ref[1, item], GROUP)
            fields, taps, bases = item_fields(got_ref, table_ref, item, channels)
            build_taps(taps[0], bases[0], row_ref, flip, origin)
            build_taps(taps[1], bases[1], col_ref, flip, 0)
            window = row_ref.shape[0]
            row_taps = row_ref[...]
            col_taps = col_ref[...].astype(jnp.bfloat16)
            for part in range(2):
                for chan in range(channels):
                    row = part * channels + chan
                    scale = fields[row : row + 1] * fields[2 * channels + chan : 2 * channels + chan + 1]
                    if flip and part == 1:
                        scale = -scale
                    weighted = (scale * row_taps).astype(jnp.bfloat16)
                    acc_ref[part, chan, pl.ds(origin, window), :] += lax.dot_general(
                        weighted,
                        col_taps,
                        (((1,), (1,)), ((), ())),
                        preferred_element_type=jnp.float32,
                    )

        return carry

    lax.fori_loop(0, items, body, 0)
    if not first:
        for part in range(2):
            total = acc_ref[part, 0]
            sym_ref[part, 0] = total.astype(jnp.bfloat16)
            for chan in range(1, channels):
                layer = acc_ref[part, chan]
                sym_ref[part, chan] = layer.astype(jnp.bfloat16)
                total = total + layer
            sum_ref[part] = total


def degrid_kernel(flags_ref, table_ref, got_ref, sym_ref, out_ref, row_ref, col_ref):
    items = got_ref.shape[0]
    channels = sym_ref.shape[1]
    out_ref[...] = jnp.zeros(out_ref.shape, jnp.float32)

    def body(item, carry):
        @pl.when(flags_ref[0, item] != 0)
        def _():
            origin = pl.multiple_of(flags_ref[1, item], GROUP)
            _, taps, bases = item_fields(got_ref, table_ref, item, channels)
            build_taps(taps[0], bases[0], row_ref, False, origin)
            build_taps(taps[1], bases[1], col_ref, False, 0)
            window = row_ref.shape[0]
            col_taps = col_ref[...].astype(jnp.bfloat16)
            row_taps = row_ref[...]
            norm = 1.0 / (TAPS * TAPS)
            for part in range(2):
                for chan in range(channels):
                    inner = jnp.dot(
                        sym_ref[part, chan, pl.ds(origin, window), :],
                        col_taps,
                        preferred_element_type=jnp.float32,
                    )
                    total = jnp.sum(row_taps * inner, axis=0, keepdims=True)
                    out_ref[item, part, pl.ds(chan, 1), :] = total * norm

        return carry

    lax.fori_loop(0, items, body, 0)


def run_grid(flags, table, got, channels, flip, acc_in=None):
    width = got.shape[2]
    vmem = pltpu.VMEM
    acc_shape = (2, channels, TS, TS)
    taps_scratch = [vmem((WINDOW, width), jnp.float32), vmem((TS, width), jnp.float32)]
    first = acc_in is None
    if first:
        out_shape = jax.ShapeDtypeStruct(acc_shape, jnp.float32)
        out_specs = pl.BlockSpec(memory_space=vmem)
        scratch = taps_scratch
        operands = (flags, table, got)
    else:
        out_shape = (
            jax.ShapeDtypeStruct((2, TS, TS), jnp.float32),
            jax.ShapeDtypeStruct(acc_shape, jnp.bfloat16),
        )
        out_specs = (pl.BlockSpec(memory_space=vmem), pl.BlockSpec(memory_space=vmem))
        scratch = [vmem(acc_shape, jnp.float32)] + taps_scratch
        operands = (flags, table, got, acc_in)
    return pl.pallas_call(
        functools.partial(grid_kernel, flip, first),
        out_shape=out_shape,
        in_specs=[pl.BlockSpec(memory_space=pltpu.SMEM)]
        + [pl.BlockSpec(memory_space=vmem) for _ in operands[1:]],
        out_specs=out_specs,
        scratch_shapes=scratch,
    )(*operands)


def run_degrid(flags, table, got, sym):
    items, _, width = got.shape
    channels = sym.shape[1]
    vmem = pltpu.VMEM
    return pl.pallas_call(
        degrid_kernel,
        out_shape=jax.ShapeDtypeStruct((items, 2, channels, width), jnp.float32),
        in_specs=[pl.BlockSpec(memory_space=pltpu.SMEM)]
        + [pl.BlockSpec(memory_space=vmem) for _ in range(3)],
        out_specs=pl.BlockSpec(memory_space=vmem),
        scratch_shapes=[vmem((WINDOW, width), jnp.float32), vmem((TS, width), jnp.float32)],
    )(flags, table, got, sym)


def slot_flags(got, channels, mirrored):
    live = got[:, 3 * channels + 4, 0] > 0
    row_base = got[:, 3 * channels].astype(jnp.int32)
    if mirrored:
        lowest = TS - TAPS - jnp.max(row_base, axis=1)
    else:
        lowest = jnp.min(row_base, axis=1)
    origin = jnp.minimum(lowest // GROUP * GROUP, TS - WINDOW)
    return jnp.stack([live.astype(jnp.int32), origin])


def per_device(visibility, imaging_weight, position, anchor, destination, block_count, kernel):
    tile_count = lax.axis_size("tile")
    mirror_bit = tile_count.bit_length() - 2
    owned_blocks, _, channels, block_width = visibility.shape
    bucket = max(2, 2 * owned_blocks // tile_count)
    slot_total = tile_count * bucket
    block_ids = jnp.arange(owned_blocks, dtype=jnp.int32)
    is_live = block_ids < block_count[0]
    same_tile = destination[:, None] == destination[None, :]
    earlier = block_ids[None, :] < block_ids[:, None]
    rank_in_tile = jnp.sum((same_tile & earlier).astype(jnp.int32), axis=1)
    slot_of = destination * bucket + rank_in_tile

    base = anchor[:, :, None] + position // OS
    offset = position % OS
    live_row = jnp.broadcast_to(is_live[:, None, None], (owned_blocks, 1, block_width))
    packed = jnp.concatenate(
        [
            visibility.reshape(owned_blocks, 2 * channels, block_width),
            imaging_weight,
            base.astype(jnp.bfloat16),
            offset.astype(jnp.bfloat16),
            live_row.astype(jnp.bfloat16),
        ],
        axis=1,
    )
    slot_ids = jnp.arange(slot_total, dtype=jnp.int32)
    matches = slot_of[None, :] == slot_ids[:, None]
    filled = jnp.any(matches, axis=1)
    source = jnp.sum(jnp.where(matches, block_ids[None, :], 0), axis=1)
    send = jnp.where(filled[:, None, None], packed[source], jnp.zeros((), jnp.bfloat16))
    got_own = lax.all_to_all(send, "tile", split_axis=0, concat_axis=0, tiled=True)
    got_other = from_partner(got_own, "tile", mirror_bit)
    table = kernel.T.astype(jnp.bfloat16)

    own_flags = slot_flags(got_own, channels, False)
    partial_grid = run_grid(own_flags, table, got_own, channels, False)
    other_flags = slot_flags(got_other, channels, True)
    grid_sum, symmetric = run_grid(other_flags, table, got_other, channels, True, partial_grid)
    combined_grid = lax.psum_scatter(grid_sum, "chan", scatter_dimension=1, tiled=True)
    own_results = run_degrid(own_flags, table, got_own, symmetric).astype(jnp.bfloat16)
    returned_slots = lax.all_to_all(own_results, "tile", split_axis=0, concat_axis=0, tiled=True)
    returned = jnp.where(
        is_live[:, None, None, None], returned_slots[slot_of], jnp.zeros((), jnp.bfloat16)
    )
    residual = (visibility.astype(jnp.float32) - returned.astype(jnp.float32)).astype(jnp.bfloat16)
    return (combined_grid, residual)


def solution(mesh):
    placed = (
        P("tile", None, "chan", None),
        P("tile", "chan", None),
        P("tile", None, None),
        P("tile", None),
        P("tile"),
        P("tile"),
        P(),
    )
    return jax.shard_map(
        per_device,
        mesh=mesh,
        in_specs=placed,
        out_specs=(P(None, ("tile", "chan"), None), P("tile", None, "chan", None)),
        check_vma=False,
    )
```

```python
import functools

import jax
import jax.numpy as jnp
from jax import lax
from jax.experimental import pallas as pl
from jax.experimental.pallas import tpu as pltpu
from jax.sharding import PartitionSpec as P

TAPS = 16
OS = 32
SUB = 128
TS = 256
GROUP = 16
WINDOW = SUB + GROUP


def from_partner(block, axis, apart):
    count = lax.axis_size(axis)
    route = []
    for low in range(count):
        high = low | 1 << apart
        if high != low and high < count:
            route += [(low, high), (high, low)]
    return lax.ppermute(block, axis, route)


def build_taps(tv, base, out_ref, flip, origin):
    rows_out, width = out_ref.shape
    if flip:
        base = TS - TAPS - base
    base = base - origin
    low_bits = base & (GROUP - 1)
    group_of = base >> 4
    rows = lax.broadcasted_iota(jnp.int32, (GROUP, width), 0)
    reach = rows - low_bits
    wrapped = reach & (GROUP - 1)
    index = TAPS - 1 - wrapped if flip else wrapped
    spread = jnp.zeros((GROUP, width), jnp.float32)
    for tap in range(TAPS):
        spread = jnp.where(index == tap, tv[tap : tap + 1, :], spread)
    placed = group_of + (reach < 0).astype(jnp.int32)
    for part in range(rows_out // GROUP):
        out_ref[pl.ds(part * GROUP, GROUP), :] = jnp.where(placed == part, spread, 0.0)


def item_fields(got_ref, table_ref, item, channels):
    fields = got_ref[item].astype(jnp.float32)
    width = fields.shape[1]
    lanes = lax.broadcasted_iota(jnp.int32, (OS, width), 0)
    table = table_ref[...]
    taps = []
    bases = []
    for axis in range(2):
        offset = fields[3 * channels + 2 + axis : 3 * channels + 3 + axis].astype(jnp.int32)
        chosen = (lanes == offset).astype(jnp.bfloat16)
        taps.append(jnp.dot(table, chosen, preferred_element_type=jnp.float32))
        bases.append(fields[3 * channels + axis : 3 * channels + 1 + axis].astype(jnp.int32))
    return fields, taps, bases


def grid_kernel(flip, first, flags_ref, table_ref, got_ref, *rest):
    if first:
        acc_ref, row_ref, col_ref = rest
        acc_ref[...] = jnp.zeros(acc_ref.shape, jnp.float32)
    else:
        acc_in_ref, sum_ref, sym_ref, acc_ref, row_ref, col_ref = rest
        acc_ref[...] = acc_in_ref[...]
    items = got_ref.shape[0]
    channels = acc_ref.shape[1]

    def body(item, carry):
        @pl.when(flags_ref[0, item] != 0)
        def _():
            origin = pl.multiple_of(flags_ref[1, item], GROUP)
            fields, taps, bases = item_fields(got_ref, table_ref, item, channels)
            build_taps(taps[0], bases[0], row_ref, flip, origin)
            build_taps(taps[1], bases[1], col_ref, flip, 0)
            window = row_ref.shape[0]
            row_taps = row_ref[...].astype(jnp.bfloat16)
            col_taps = col_ref[...]
            for part in range(2):
                for chan in range(channels):
                    row = part * channels + chan
                    scale = fields[row : row + 1] * fields[2 * channels + chan : 2 * channels + chan + 1]
                    if flip and part == 1:
                        scale = -scale
                    weighted = (scale * col_taps).astype(jnp.bfloat16)
                    acc_ref[part, chan, pl.ds(origin, window), :] += lax.dot_general(
                        row_taps,
                        weighted,
                        (((1,), (1,)), ((), ())),
                        preferred_element_type=jnp.float32,
                    )

        return carry

    lax.fori_loop(0, items, body, 0)
    if not first:
        for part in range(2):
            total = acc_ref[part, 0]
            sym_ref[part, 0] = total.astype(jnp.bfloat16)
            for chan in range(1, channels):
                layer = acc_ref[part, chan]
                sym_ref[part, chan] = layer.astype(jnp.bfloat16)
                total = total + layer
            sum_ref[part] = total


def degrid_kernel(flags_ref, table_ref, got_ref, sym_ref, out_ref, row_ref, col_ref):
    items = got_ref.shape[0]
    channels = sym_ref.shape[1]
    out_ref[...] = jnp.zeros(out_ref.shape, jnp.float32)

    def body(item, carry):
        @pl.when(flags_ref[0, item] != 0)
        def _():
            origin = pl.multiple_of(flags_ref[1, item], GROUP)
            _, taps, bases = item_fields(got_ref, table_ref, item, channels)
            build_taps(taps[0], bases[0], row_ref, False, origin)
            build_taps(taps[1], bases[1], col_ref, False, 0)
            window = row_ref.shape[0]
            col_taps = col_ref[...].astype(jnp.bfloat16)
            row_taps = row_ref[...]
            norm = 1.0 / (TAPS * TAPS)
            for part in range(2):
                for chan in range(channels):
                    inner = jnp.dot(
                        sym_ref[part, chan, pl.ds(origin, window), :],
                        col_taps,
                        preferred_element_type=jnp.float32,
                    )
                    total = jnp.sum(row_taps * inner, axis=0, keepdims=True)
                    out_ref[item, part, pl.ds(chan, 1), :] = total * norm

        return carry

    lax.fori_loop(0, items, body, 0)


def run_grid(flags, table, got, channels, flip, acc_in=None):
    width = got.shape[2]
    vmem = pltpu.VMEM
    acc_shape = (2, channels, TS, TS)
    taps_scratch = [vmem((WINDOW, width), jnp.float32), vmem((TS, width), jnp.float32)]
    first = acc_in is None
    if first:
        out_shape = jax.ShapeDtypeStruct(acc_shape, jnp.float32)
        out_specs = pl.BlockSpec(memory_space=vmem)
        scratch = taps_scratch
        operands = (flags, table, got)
    else:
        out_shape = (
            jax.ShapeDtypeStruct((2, TS, TS), jnp.float32),
            jax.ShapeDtypeStruct(acc_shape, jnp.bfloat16),
        )
        out_specs = (pl.BlockSpec(memory_space=vmem), pl.BlockSpec(memory_space=vmem))
        scratch = [vmem(acc_shape, jnp.float32)] + taps_scratch
        operands = (flags, table, got, acc_in)
    return pl.pallas_call(
        functools.partial(grid_kernel, flip, first),
        out_shape=out_shape,
        in_specs=[pl.BlockSpec(memory_space=pltpu.SMEM)]
        + [pl.BlockSpec(memory_space=vmem) for _ in operands[1:]],
        out_specs=out_specs,
        scratch_shapes=scratch,
    )(*operands)


def run_degrid(flags, table, got, sym):
    items, _, width = got.shape
    channels = sym.shape[1]
    vmem = pltpu.VMEM
    return pl.pallas_call(
        degrid_kernel,
        out_shape=jax.ShapeDtypeStruct((items, 2, channels, width), jnp.float32),
        in_specs=[pl.BlockSpec(memory_space=pltpu.SMEM)]
        + [pl.BlockSpec(memory_space=vmem) for _ in range(3)],
        out_specs=pl.BlockSpec(memory_space=vmem),
        scratch_shapes=[vmem((WINDOW, width), jnp.float32), vmem((TS, width), jnp.float32)],
    )(flags, table, got, sym)


def slot_flags(got, channels, mirrored):
    live = got[:, 3 * channels + 4, 0] > 0
    row_base = got[:, 3 * channels].astype(jnp.int32)
    if mirrored:
        lowest = TS - TAPS - jnp.max(row_base, axis=1)
    else:
        lowest = jnp.min(row_base, axis=1)
    origin = jnp.minimum(lowest // GROUP * GROUP, TS - WINDOW)
    return jnp.stack([live.astype(jnp.int32), origin])


def per_device(visibility, imaging_weight, position, anchor, destination, block_count, kernel):
    tile_count = lax.axis_size("tile")
    mirror_bit = tile_count.bit_length() - 2
    owned_blocks, _, channels, block_width = visibility.shape
    bucket = max(2, 2 * owned_blocks // tile_count)
    slot_total = tile_count * bucket
    block_ids = jnp.arange(owned_blocks, dtype=jnp.int32)
    is_live = block_ids < block_count[0]
    same_tile = destination[:, None] == destination[None, :]
    earlier = block_ids[None, :] < block_ids[:, None]
    rank_in_tile = jnp.sum((same_tile & earlier).astype(jnp.int32), axis=1)
    slot_of = destination * bucket + rank_in_tile

    base = anchor[:, :, None] + position // OS
    offset = position % OS
    live_row = jnp.broadcast_to(is_live[:, None, None], (owned_blocks, 1, block_width))
    packed = jnp.concatenate(
        [
            visibility.reshape(owned_blocks, 2 * channels, block_width),
            imaging_weight,
            base.astype(jnp.bfloat16),
            offset.astype(jnp.bfloat16),
            live_row.astype(jnp.bfloat16),
        ],
        axis=1,
    )
    slot_ids = jnp.arange(slot_total, dtype=jnp.int32)
    matches = slot_of[None, :] == slot_ids[:, None]
    filled = jnp.any(matches, axis=1)
    source = jnp.sum(jnp.where(matches, block_ids[None, :], 0), axis=1)
    send = jnp.where(filled[:, None, None], packed[source], jnp.zeros((), jnp.bfloat16))
    got_own = lax.all_to_all(send, "tile", split_axis=0, concat_axis=0, tiled=True)
    got_other = from_partner(got_own, "tile", mirror_bit)
    table = kernel.T.astype(jnp.bfloat16)

    own_flags = slot_flags(got_own, channels, False)
    partial_grid = run_grid(own_flags, table, got_own, channels, False)
    other_flags = slot_flags(got_other, channels, True)
    grid_sum, symmetric = run_grid(other_flags, table, got_other, channels, True, partial_grid)
    combined_grid = lax.psum_scatter(grid_sum, "chan", scatter_dimension=1, tiled=True)
    own_results = run_degrid(own_flags, table, got_own, symmetric).astype(jnp.bfloat16)
    returned_slots = lax.all_to_all(own_results, "tile", split_axis=0, concat_axis=0, tiled=True)
    returned = jnp.where(
        is_live[:, None, None, None], returned_slots[slot_of], jnp.zeros((), jnp.bfloat16)
    )
    residual = (visibility.astype(jnp.float32) - returned.astype(jnp.float32)).astype(jnp.bfloat16)
    return (combined_grid, residual)


def solution(mesh):
    placed = (
        P("tile", None, "chan", None),
        P("tile", "chan", None),
        P("tile", None, None),
        P("tile", None),
        P("tile"),
        P("tile"),
        P(),
    )
    return jax.shard_map(
        per_device,
        mesh=mesh,
        in_specs=placed,
        out_specs=(P(None, ("tile", "chan"), None), P("tile", None, "chan", None)),
        check_vma=False,
    )
```

```python
import functools

import jax
import jax.numpy as jnp
from jax import lax
from jax.experimental import pallas as pl
from jax.experimental.pallas import tpu as pltpu
from jax.sharding import PartitionSpec as P

TAPS = 16
OS = 32
SUB = 128
TS = 256
GROUP = 16
WINDOW = SUB + GROUP


def from_partner(block, axis, apart):
    count = lax.axis_size(axis)
    route = []
    for low in range(count):
        high = low | 1 << apart
        if high != low and high < count:
            route += [(low, high), (high, low)]
    return lax.ppermute(block, axis, route)


def build_taps(tv, base, out_ref, flip, origin):
    rows_out, width = out_ref.shape
    if flip:
        base = TS - TAPS - base
    base = base - origin
    low_bits = base & (GROUP - 1)
    group_of = base >> 4
    rows = lax.broadcasted_iota(jnp.int32, (GROUP, width), 0)
    reach = rows - low_bits
    wrapped = reach & (GROUP - 1)
    index = TAPS - 1 - wrapped if flip else wrapped
    spread = jnp.zeros((GROUP, width), jnp.float32)
    for tap in range(TAPS):
        spread = jnp.where(index == tap, tv[tap : tap + 1, :], spread)
    placed = group_of + (reach < 0).astype(jnp.int32)
    for part in range(rows_out // GROUP):
        out_ref[pl.ds(part * GROUP, GROUP), :] = jnp.where(placed == part, spread, 0.0)


def item_fields(got_ref, table_ref, item, channels):
    fields = got_ref[item].astype(jnp.float32)
    width = fields.shape[1]
    lanes = lax.broadcasted_iota(jnp.int32, (OS, width), 0)
    table = table_ref[...]
    taps = []
    bases = []
    for axis in range(2):
        offset = fields[3 * channels + 2 + axis : 3 * channels + 3 + axis].astype(jnp.int32)
        chosen = (lanes == offset).astype(jnp.bfloat16)
        taps.append(jnp.dot(table, chosen, preferred_element_type=jnp.float32))
        bases.append(fields[3 * channels + axis : 3 * channels + 1 + axis].astype(jnp.int32))
    return fields, taps, bases


def grid_kernel(flip, first, flags_ref, table_ref, got_ref, *rest):
    if first:
        acc_ref, row_ref, col_ref = rest
        acc_ref[...] = jnp.zeros(acc_ref.shape, jnp.float32)
    else:
        acc_in_ref, sum_ref, sym_ref, acc_ref, row_ref, col_ref = rest
        acc_ref[...] = acc_in_ref[...]
    items = got_ref.shape[0]
    channels = acc_ref.shape[1]

    def body(item, carry):
        @pl.when(flags_ref[0, item] != 0)
        def _():
            origin = pl.multiple_of(flags_ref[1, item], GROUP)
            fields, taps, bases = item_fields(got_ref, table_ref, item, channels)
            build_taps(taps[0], bases[0], row_ref, flip, origin)
            build_taps(taps[1], bases[1], col_ref, flip, 0)
            window = row_ref.shape[0]
            row_taps = row_ref[...].astype(jnp.bfloat16)
            col_taps = col_ref[...]
            for part in range(2):
                for chan in range(channels):
                    row = part * channels + chan
                    scale = fields[row : row + 1] * fields[2 * channels + chan : 2 * channels + chan + 1]
                    if flip and part == 1:
                        scale = -scale
                    weighted = (scale * col_taps).astype(jnp.bfloat16)
                    acc_ref[part, chan, pl.ds(origin, window), :] += lax.dot_general(
                        row_taps,
                        weighted,
                        (((1,), (1,)), ((), ())),
                        preferred_element_type=jnp.float32,
                    )

        return carry

    lax.fori_loop(0, items, body, 0)
    if not first:
        for part in range(2):
            total = acc_ref[part, 0]
            sym_ref[part, 0] = total.astype(jnp.bfloat16)
            for chan in range(1, channels):
                layer = acc_ref[part, chan]
                sym_ref[part, chan] = layer.astype(jnp.bfloat16)
                total = total + layer
            sum_ref[part] = total


def degrid_kernel(flags_ref, table_ref, got_ref, sym_ref, out_ref, row_ref, col_ref):
    items = got_ref.shape[0]
    channels = sym_ref.shape[1]
    out_ref[...] = jnp.zeros(out_ref.shape, out_ref.dtype)

    def body(item, carry):
        @pl.when(flags_ref[0, item] != 0)
        def _():
            origin = pl.multiple_of(flags_ref[1, item], GROUP)
            _, taps, bases = item_fields(got_ref, table_ref, item, channels)
            build_taps(taps[0], bases[0], row_ref, False, origin)
            build_taps(taps[1], bases[1], col_ref, False, 0)
            window = row_ref.shape[0]
            col_taps = col_ref[...].astype(jnp.bfloat16)
            row_taps = row_ref[...]
            norm = 1.0 / (TAPS * TAPS)
            for part in range(2):
                rows = []
                for chan in range(channels):
                    inner = jnp.dot(
                        sym_ref[part, chan, pl.ds(origin, window), :],
                        col_taps,
                        preferred_element_type=jnp.float32,
                    )
                    rows.append(jnp.sum(row_taps * inner, axis=0, keepdims=True) * norm)
                out_ref[item, part] = jnp.concatenate(rows, axis=0).astype(out_ref.dtype)

        return carry

    lax.fori_loop(0, items, body, 0)


def run_grid(flags, table, got, channels, flip, acc_in=None):
    width = got.shape[2]
    vmem = pltpu.VMEM
    acc_shape = (2, channels, TS, TS)
    taps_scratch = [vmem((WINDOW, width), jnp.float32), vmem((TS, width), jnp.float32)]
    first = acc_in is None
    if first:
        out_shape = jax.ShapeDtypeStruct(acc_shape, jnp.float32)
        out_specs = pl.BlockSpec(memory_space=vmem)
        scratch = taps_scratch
        operands = (flags, table, got)
    else:
        out_shape = (
            jax.ShapeDtypeStruct((2, TS, TS), jnp.float32),
            jax.ShapeDtypeStruct(acc_shape, jnp.bfloat16),
        )
        out_specs = (pl.BlockSpec(memory_space=vmem), pl.BlockSpec(memory_space=vmem))
        scratch = [vmem(acc_shape, jnp.float32)] + taps_scratch
        operands = (flags, table, got, acc_in)
    return pl.pallas_call(
        functools.partial(grid_kernel, flip, first),
        out_shape=out_shape,
        in_specs=[pl.BlockSpec(memory_space=pltpu.SMEM)]
        + [pl.BlockSpec(memory_space=vmem) for _ in operands[1:]],
        out_specs=out_specs,
        scratch_shapes=scratch,
    )(*operands)


def run_degrid(flags, table, got, sym):
    items, _, width = got.shape
    channels = sym.shape[1]
    vmem = pltpu.VMEM
    return pl.pallas_call(
        degrid_kernel,
        out_shape=jax.ShapeDtypeStruct((items, 2, channels, width), jnp.bfloat16),
        in_specs=[pl.BlockSpec(memory_space=pltpu.SMEM)]
        + [pl.BlockSpec(memory_space=vmem) for _ in range(3)],
        out_specs=pl.BlockSpec(memory_space=vmem),
        scratch_shapes=[vmem((WINDOW, width), jnp.float32), vmem((TS, width), jnp.float32)],
    )(flags, table, got, sym)


def slot_flags(got, channels, mirrored):
    live = got[:, 3 * channels + 4, 0] > 0
    row_base = got[:, 3 * channels].astype(jnp.int32)
    if mirrored:
        lowest = TS - TAPS - jnp.max(row_base, axis=1)
    else:
        lowest = jnp.min(row_base, axis=1)
    origin = jnp.minimum(lowest // GROUP * GROUP, TS - WINDOW)
    return jnp.stack([live.astype(jnp.int32), origin])


def per_device(visibility, imaging_weight, position, anchor, destination, block_count, kernel):
    tile_count = lax.axis_size("tile")
    mirror_bit = tile_count.bit_length() - 2
    owned_blocks, _, channels, block_width = visibility.shape
    bucket = max(2, 2 * owned_blocks // tile_count)
    slot_total = tile_count * bucket
    block_ids = jnp.arange(owned_blocks, dtype=jnp.int32)
    is_live = block_ids < block_count[0]
    same_tile = destination[:, None] == destination[None, :]
    earlier = block_ids[None, :] < block_ids[:, None]
    rank_in_tile = jnp.sum((same_tile & earlier).astype(jnp.int32), axis=1)
    slot_of = destination * bucket + rank_in_tile

    base = anchor[:, :, None] + position // OS
    offset = position % OS
    live_row = jnp.broadcast_to(is_live[:, None, None], (owned_blocks, 1, block_width))
    packed = jnp.concatenate(
        [
            visibility.reshape(owned_blocks, 2 * channels, block_width),
            imaging_weight,
            base.astype(jnp.bfloat16),
            offset.astype(jnp.bfloat16),
            live_row.astype(jnp.bfloat16),
        ],
        axis=1,
    )
    slot_ids = jnp.arange(slot_total, dtype=jnp.int32)
    matches = slot_of[None, :] == slot_ids[:, None]
    filled = jnp.any(matches, axis=1)
    source = jnp.sum(jnp.where(matches, block_ids[None, :], 0), axis=1)
    send = jnp.where(filled[:, None, None], packed[source], jnp.zeros((), jnp.bfloat16))
    got_own = lax.all_to_all(send, "tile", split_axis=0, concat_axis=0, tiled=True)
    got_other = from_partner(got_own, "tile", mirror_bit)
    table = kernel.T.astype(jnp.bfloat16)

    own_flags = slot_flags(got_own, channels, False)
    partial_grid = run_grid(own_flags, table, got_own, channels, False)
    other_flags = slot_flags(got_other, channels, True)
    grid_sum, symmetric = run_grid(other_flags, table, got_other, channels, True, partial_grid)
    combined_grid = lax.psum_scatter(grid_sum, "chan", scatter_dimension=1, tiled=True)
    own_results = run_degrid(own_flags, table, got_own, symmetric)
    returned_slots = lax.all_to_all(own_results, "tile", split_axis=0, concat_axis=0, tiled=True)
    returned = jnp.where(
        is_live[:, None, None, None], returned_slots[slot_of], jnp.zeros((), jnp.bfloat16)
    )
    residual = (visibility.astype(jnp.float32) - returned.astype(jnp.float32)).astype(jnp.bfloat16)
    return (combined_grid, residual)


def solution(mesh):
    placed = (
        P("tile", None, "chan", None),
        P("tile", "chan", None),
        P("tile", None, None),
        P("tile", None),
        P("tile"),
        P("tile"),
        P(),
    )
    return jax.shard_map(
        per_device,
        mesh=mesh,
        in_specs=placed,
        out_specs=(P(None, ("tile", "chan"), None), P("tile", None, "chan", None)),
        check_vma=False,
    )
```

```python
import functools

import jax
import jax.numpy as jnp
from jax import lax
from jax.experimental import pallas as pl
from jax.experimental.pallas import tpu as pltpu
from jax.sharding import PartitionSpec as P

TAPS = 16
OS = 32
SUB = 128
TS = 256
GROUP = 16
WINDOW = SUB + GROUP


def from_partner(block, axis, apart):
    count = lax.axis_size(axis)
    route = []
    for low in range(count):
        high = low | 1 << apart
        if high != low and high < count:
            route += [(low, high), (high, low)]
    return lax.ppermute(block, axis, route)


def build_taps(tv, base, out_ref, flip, origin):
    rows_out, width = out_ref.shape
    if flip:
        base = TS - TAPS - base
    base = base - origin
    low_bits = base & (GROUP - 1)
    group_of = base >> 4
    rows = lax.broadcasted_iota(jnp.int32, (GROUP, width), 0)
    reach = rows - low_bits
    wrapped = reach & (GROUP - 1)
    index = TAPS - 1 - wrapped if flip else wrapped
    level = [tv[tap : tap + 1, :] for tap in range(TAPS)]
    bit = 1
    while len(level) > 1:
        upper_half = (index & bit) != 0
        level = [jnp.where(upper_half, level[k + 1], level[k]) for k in range(0, len(level), 2)]
        bit *= 2
    spread = level[0]
    placed = group_of + (reach < 0).astype(jnp.int32)
    for part in range(rows_out // GROUP):
        out_ref[pl.ds(part * GROUP, GROUP), :] = jnp.where(placed == part, spread, 0.0)


def item_fields(got_ref, table_ref, item, channels):
    fields = got_ref[item].astype(jnp.float32)
    width = fields.shape[1]
    lanes = lax.broadcasted_iota(jnp.int32, (OS, width), 0)
    table = table_ref[...]
    taps = []
    bases = []
    for axis in range(2):
        offset = fields[3 * channels + 2 + axis : 3 * channels + 3 + axis].astype(jnp.int32)
        chosen = (lanes == offset).astype(jnp.bfloat16)
        taps.append(jnp.dot(table, chosen, preferred_element_type=jnp.float32))
        bases.append(fields[3 * channels + axis : 3 * channels + 1 + axis].astype(jnp.int32))
    return fields, taps, bases


def grid_kernel(flip, first, flags_ref, table_ref, got_ref, *rest):
    if first:
        acc_ref, row_ref, col_ref = rest
        acc_ref[...] = jnp.zeros(acc_ref.shape, jnp.float32)
    else:
        acc_in_ref, sum_ref, sym_ref, acc_ref, row_ref, col_ref = rest
        acc_ref[...] = acc_in_ref[...]
    items = got_ref.shape[0]
    channels = acc_ref.shape[1]

    def body(item, carry):
        @pl.when(flags_ref[0, item] != 0)
        def _():
            origin = pl.multiple_of(flags_ref[1, item], GROUP)
            fields, taps, bases = item_fields(got_ref, table_ref, item, channels)
            build_taps(taps[0], bases[0], row_ref, flip, origin)
            build_taps(taps[1], bases[1], col_ref, flip, 0)
            window = row_ref.shape[0]
            row_taps = row_ref[...].astype(jnp.bfloat16)
            col_taps = col_ref[...]
            for part in range(2):
                for chan in range(channels):
                    row = part * channels + chan
                    scale = fields[row : row + 1] * fields[2 * channels + chan : 2 * channels + chan + 1]
                    if flip and part == 1:
                        scale = -scale
                    weighted = (scale * col_taps).astype(jnp.bfloat16)
                    acc_ref[part, chan, pl.ds(origin, window), :] += lax.dot_general(
                        row_taps,
                        weighted,
                        (((1,), (1,)), ((), ())),
                        preferred_element_type=jnp.float32,
                    )

        return carry

    lax.fori_loop(0, items, body, 0)
    if not first:
        for part in range(2):
            total = acc_ref[part, 0]
            sym_ref[part, 0] = total.astype(jnp.bfloat16)
            for chan in range(1, channels):
                layer = acc_ref[part, chan]
                sym_ref[part, chan] = layer.astype(jnp.bfloat16)
                total = total + layer
            sum_ref[part] = total


def degrid_kernel(flags_ref, table_ref, got_ref, sym_ref, out_ref, row_ref, col_ref):
    items = got_ref.shape[0]
    channels = sym_ref.shape[1]
    out_ref[...] = jnp.zeros(out_ref.shape, out_ref.dtype)

    def body(item, carry):
        @pl.when(flags_ref[0, item] != 0)
        def _():
            origin = pl.multiple_of(flags_ref[1, item], GROUP)
            _, taps, bases = item_fields(got_ref, table_ref, item, channels)
            build_taps(taps[0], bases[0], row_ref, False, origin)
            build_taps(taps[1], bases[1], col_ref, False, 0)
            window = row_ref.shape[0]
            col_taps = col_ref[...].astype(jnp.bfloat16)
            row_taps = row_ref[...]
            norm = 1.0 / (TAPS * TAPS)
            for part in range(2):
                rows = []
                for chan in range(channels):
                    inner = jnp.dot(
                        sym_ref[part, chan, pl.ds(origin, window), :],
                        col_taps,
                        preferred_element_type=jnp.float32,
                    )
                    rows.append(jnp.sum(row_taps * inner, axis=0, keepdims=True) * norm)
                out_ref[item, part] = jnp.concatenate(rows, axis=0).astype(out_ref.dtype)

        return carry

    lax.fori_loop(0, items, body, 0)


def run_grid(flags, table, got, channels, flip, acc_in=None):
    width = got.shape[2]
    vmem = pltpu.VMEM
    acc_shape = (2, channels, TS, TS)
    taps_scratch = [vmem((WINDOW, width), jnp.float32), vmem((TS, width), jnp.float32)]
    first = acc_in is None
    if first:
        out_shape = jax.ShapeDtypeStruct(acc_shape, jnp.float32)
        out_specs = pl.BlockSpec(memory_space=vmem)
        scratch = taps_scratch
        operands = (flags, table, got)
    else:
        out_shape = (
            jax.ShapeDtypeStruct((2, TS, TS), jnp.float32),
            jax.ShapeDtypeStruct(acc_shape, jnp.bfloat16),
        )
        out_specs = (pl.BlockSpec(memory_space=vmem), pl.BlockSpec(memory_space=vmem))
        scratch = [vmem(acc_shape, jnp.float32)] + taps_scratch
        operands = (flags, table, got, acc_in)
    return pl.pallas_call(
        functools.partial(grid_kernel, flip, first),
        out_shape=out_shape,
        in_specs=[pl.BlockSpec(memory_space=pltpu.SMEM)]
        + [pl.BlockSpec(memory_space=vmem) for _ in operands[1:]],
        out_specs=out_specs,
        scratch_shapes=scratch,
    )(*operands)


def run_degrid(flags, table, got, sym):
    items, _, width = got.shape
    channels = sym.shape[1]
    vmem = pltpu.VMEM
    return pl.pallas_call(
        degrid_kernel,
        out_shape=jax.ShapeDtypeStruct((items, 2, channels, width), jnp.bfloat16),
        in_specs=[pl.BlockSpec(memory_space=pltpu.SMEM)]
        + [pl.BlockSpec(memory_space=vmem) for _ in range(3)],
        out_specs=pl.BlockSpec(memory_space=vmem),
        scratch_shapes=[vmem((WINDOW, width), jnp.float32), vmem((TS, width), jnp.float32)],
    )(flags, table, got, sym)


def slot_flags(got, channels, mirrored):
    live = got[:, 3 * channels + 4, 0] > 0
    row_base = got[:, 3 * channels].astype(jnp.int32)
    if mirrored:
        lowest = TS - TAPS - jnp.max(row_base, axis=1)
    else:
        lowest = jnp.min(row_base, axis=1)
    origin = jnp.minimum(lowest // GROUP * GROUP, TS - WINDOW)
    return jnp.stack([live.astype(jnp.int32), origin])


def per_device(visibility, imaging_weight, position, anchor, destination, block_count, kernel):
    tile_count = lax.axis_size("tile")
    mirror_bit = tile_count.bit_length() - 2
    owned_blocks, _, channels, block_width = visibility.shape
    bucket = max(2, 2 * owned_blocks // tile_count)
    slot_total = tile_count * bucket
    block_ids = jnp.arange(owned_blocks, dtype=jnp.int32)
    is_live = block_ids < block_count[0]
    same_tile = destination[:, None] == destination[None, :]
    earlier = block_ids[None, :] < block_ids[:, None]
    rank_in_tile = jnp.sum((same_tile & earlier).astype(jnp.int32), axis=1)
    slot_of = destination * bucket + rank_in_tile

    base = anchor[:, :, None] + position // OS
    offset = position % OS
    live_row = jnp.broadcast_to(is_live[:, None, None], (owned_blocks, 1, block_width))
    packed = jnp.concatenate(
        [
            visibility[:, 0],
            visibility[:, 1],
            imaging_weight,
            base.astype(jnp.bfloat16),
            offset.astype(jnp.bfloat16),
            live_row.astype(jnp.bfloat16),
        ],
        axis=1,
    )
    slot_ids = jnp.arange(slot_total, dtype=jnp.int32)
    matches = slot_of[None, :] == slot_ids[:, None]
    filled = jnp.any(matches, axis=1)
    source = jnp.sum(jnp.where(matches, block_ids[None, :], 0), axis=1)
    send = jnp.where(filled[:, None, None], packed[source], jnp.zeros((), jnp.bfloat16))
    got_own = lax.all_to_all(send, "tile", split_axis=0, concat_axis=0, tiled=True)
    got_other = from_partner(got_own, "tile", mirror_bit)
    table = kernel.T.astype(jnp.bfloat16)

    own_flags = slot_flags(got_own, channels, False)
    partial_grid = run_grid(own_flags, table, got_own, channels, False)
    other_flags = slot_flags(got_other, channels, True)
    grid_sum, symmetric = run_grid(other_flags, table, got_other, channels, True, partial_grid)
    combined_grid = lax.psum_scatter(grid_sum, "chan", scatter_dimension=1, tiled=True)
    own_results = run_degrid(own_flags, table, got_own, symmetric)
    returned_slots = lax.all_to_all(own_results, "tile", split_axis=0, concat_axis=0, tiled=True)
    returned = jnp.where(
        is_live[:, None, None, None], returned_slots[slot_of], jnp.zeros((), jnp.bfloat16)
    )
    residual = (visibility.astype(jnp.float32) - returned.astype(jnp.float32)).astype(jnp.bfloat16)
    return (combined_grid, residual)


def solution(mesh):
    placed = (
        P("tile", None, "chan", None),
        P("tile", "chan", None),
        P("tile", None, None),
        P("tile", None),
        P("tile"),
        P("tile"),
        P(),
    )
    return jax.shard_map(
        per_device,
        mesh=mesh,
        in_specs=placed,
        out_specs=(P(None, ("tile", "chan"), None), P("tile", None, "chan", None)),
        check_vma=False,
    )
```

```python
import functools

import jax
import jax.numpy as jnp
from jax import lax
from jax.experimental import pallas as pl
from jax.experimental.pallas import tpu as pltpu
from jax.sharding import PartitionSpec as P

TAPS = 16
OS = 32
SUB = 128
TS = 256
GROUP = 16
WINDOW = SUB + GROUP


def from_partner(block, axis, apart):
    count = lax.axis_size(axis)
    route = []
    for low in range(count):
        high = low | 1 << apart
        if high != low and high < count:
            route += [(low, high), (high, low)]
    return lax.ppermute(block, axis, route)


def build_taps(tv, base, out_ref, flip, origin):
    rows_out, width = out_ref.shape
    if flip:
        base = TS - TAPS - base
    base = base - origin
    low_bits = base & (GROUP - 1)
    group_of = base >> 4
    rows = lax.broadcasted_iota(jnp.int32, (GROUP, width), 0)
    reach = rows - low_bits
    wrapped = reach & (GROUP - 1)
    index = TAPS - 1 - wrapped if flip else wrapped
    level = [tv[tap : tap + 1, :] for tap in range(TAPS)]
    bit = 1
    while len(level) > 1:
        upper_half = (index & bit) != 0
        level = [jnp.where(upper_half, level[k + 1], level[k]) for k in range(0, len(level), 2)]
        bit *= 2
    spread = level[0]
    placed = group_of + (reach < 0).astype(jnp.int32)
    for part in range(rows_out // GROUP):
        out_ref[pl.ds(part * GROUP, GROUP), :] = jnp.where(placed == part, spread, 0.0)


def item_fields(got_ref, table_ref, item, channels):
    fields = got_ref[item].astype(jnp.float32)
    width = fields.shape[1]
    lanes = lax.broadcasted_iota(jnp.int32, (OS, width), 0)
    table = table_ref[...]
    taps = []
    bases = []
    for axis in range(2):
        offset = fields[3 * channels + 2 + axis : 3 * channels + 3 + axis].astype(jnp.int32)
        chosen = (lanes == offset).astype(jnp.bfloat16)
        taps.append(jnp.dot(table, chosen, preferred_element_type=jnp.float32))
        bases.append(fields[3 * channels + axis : 3 * channels + 1 + axis].astype(jnp.int32))
    return fields, taps, bases


def grid_kernel(flip, first, flags_ref, table_ref, got_ref, *rest):
    if first:
        acc_ref, row_ref, col_ref = rest
        acc_ref[...] = jnp.zeros(acc_ref.shape, jnp.float32)
    else:
        acc_in_ref, sum_ref, sym_ref, acc_ref, row_ref, col_ref = rest
        acc_ref[...] = acc_in_ref[...]
    items = got_ref.shape[0]
    channels = acc_ref.shape[1]

    def body(item, carry):
        @pl.when(flags_ref[0, item] != 0)
        def _():
            origin = pl.multiple_of(flags_ref[1, item], GROUP)
            fields, taps, bases = item_fields(got_ref, table_ref, item, channels)
            build_taps(taps[0], bases[0], row_ref, flip, origin)
            build_taps(taps[1], bases[1], col_ref, flip, 0)
            window = row_ref.shape[0]
            row_taps = row_ref[...].astype(jnp.bfloat16)
            col_taps = col_ref[...]
            for part in range(2):
                for chan in range(channels):
                    row = part * channels + chan
                    scale = fields[row : row + 1] * fields[2 * channels + chan : 2 * channels + chan + 1]
                    if flip and part == 1:
                        scale = -scale
                    weighted = (scale * col_taps).astype(jnp.bfloat16)
                    acc_ref[part, chan, pl.ds(origin, window), :] += lax.dot_general(
                        row_taps,
                        weighted,
                        (((1,), (1,)), ((), ())),
                        preferred_element_type=jnp.float32,
                    )

        return carry

    lax.fori_loop(0, items, body, 0, unroll=2)
    if not first:
        for part in range(2):
            total = acc_ref[part, 0]
            sym_ref[part, 0] = total.astype(jnp.bfloat16)
            for chan in range(1, channels):
                layer = acc_ref[part, chan]
                sym_ref[part, chan] = layer.astype(jnp.bfloat16)
                total = total + layer
            sum_ref[part] = total


def degrid_kernel(flags_ref, table_ref, got_ref, sym_ref, out_ref, row_ref, col_ref):
    items = got_ref.shape[0]
    channels = sym_ref.shape[1]
    out_ref[...] = jnp.zeros(out_ref.shape, out_ref.dtype)

    def body(item, carry):
        @pl.when(flags_ref[0, item] != 0)
        def _():
            origin = pl.multiple_of(flags_ref[1, item], GROUP)
            _, taps, bases = item_fields(got_ref, table_ref, item, channels)
            build_taps(taps[0], bases[0], row_ref, False, origin)
            build_taps(taps[1], bases[1], col_ref, False, 0)
            window = row_ref.shape[0]
            col_taps = col_ref[...].astype(jnp.bfloat16)
            row_taps = row_ref[...]
            norm = 1.0 / (TAPS * TAPS)
            for part in range(2):
                rows = []
                for chan in range(channels):
                    inner = jnp.dot(
                        sym_ref[part, chan, pl.ds(origin, window), :],
                        col_taps,
                        preferred_element_type=jnp.float32,
                    )
                    rows.append(jnp.sum(row_taps * inner, axis=0, keepdims=True) * norm)
                out_ref[item, part] = jnp.concatenate(rows, axis=0).astype(out_ref.dtype)

        return carry

    lax.fori_loop(0, items, body, 0, unroll=2)


def run_grid(flags, table, got, channels, flip, acc_in=None):
    width = got.shape[2]
    vmem = pltpu.VMEM
    acc_shape = (2, channels, TS, TS)
    taps_scratch = [vmem((WINDOW, width), jnp.float32), vmem((TS, width), jnp.float32)]
    first = acc_in is None
    if first:
        out_shape = jax.ShapeDtypeStruct(acc_shape, jnp.float32)
        out_specs = pl.BlockSpec(memory_space=vmem)
        scratch = taps_scratch
        operands = (flags, table, got)
    else:
        out_shape = (
            jax.ShapeDtypeStruct((2, TS, TS), jnp.float32),
            jax.ShapeDtypeStruct(acc_shape, jnp.bfloat16),
        )
        out_specs = (pl.BlockSpec(memory_space=vmem), pl.BlockSpec(memory_space=vmem))
        scratch = [vmem(acc_shape, jnp.float32)] + taps_scratch
        operands = (flags, table, got, acc_in)
    return pl.pallas_call(
        functools.partial(grid_kernel, flip, first),
        out_shape=out_shape,
        in_specs=[pl.BlockSpec(memory_space=pltpu.SMEM)]
        + [pl.BlockSpec(memory_space=vmem) for _ in operands[1:]],
        out_specs=out_specs,
        scratch_shapes=scratch,
    )(*operands)


def run_degrid(flags, table, got, sym):
    items, _, width = got.shape
    channels = sym.shape[1]
    vmem = pltpu.VMEM
    return pl.pallas_call(
        degrid_kernel,
        out_shape=jax.ShapeDtypeStruct((items, 2, channels, width), jnp.bfloat16),
        in_specs=[pl.BlockSpec(memory_space=pltpu.SMEM)]
        + [pl.BlockSpec(memory_space=vmem) for _ in range(3)],
        out_specs=pl.BlockSpec(memory_space=vmem),
        scratch_shapes=[vmem((WINDOW, width), jnp.float32), vmem((TS, width), jnp.float32)],
    )(flags, table, got, sym)


def slot_flags(got, channels, mirrored):
    live = got[:, 3 * channels + 4, 0] > 0
    row_base = got[:, 3 * channels].astype(jnp.int32)
    if mirrored:
        lowest = TS - TAPS - jnp.max(row_base, axis=1)
    else:
        lowest = jnp.min(row_base, axis=1)
    origin = jnp.minimum(lowest // GROUP * GROUP, TS - WINDOW)
    return jnp.stack([live.astype(jnp.int32), origin])


def per_device(visibility, imaging_weight, position, anchor, destination, block_count, kernel):
    tile_count = lax.axis_size("tile")
    mirror_bit = tile_count.bit_length() - 2
    owned_blocks, _, channels, block_width = visibility.shape
    bucket = max(2, 2 * owned_blocks // tile_count)
    slot_total = tile_count * bucket
    block_ids = jnp.arange(owned_blocks, dtype=jnp.int32)
    is_live = block_ids < block_count[0]
    same_tile = destination[:, None] == destination[None, :]
    earlier = block_ids[None, :] < block_ids[:, None]
    rank_in_tile = jnp.sum((same_tile & earlier).astype(jnp.int32), axis=1)
    slot_of = destination * bucket + rank_in_tile

    base = anchor[:, :, None] + position // OS
    offset = position % OS
    live_row = jnp.broadcast_to(is_live[:, None, None], (owned_blocks, 1, block_width))
    packed = jnp.concatenate(
        [
            visibility[:, 0],
            visibility[:, 1],
            imaging_weight,
            base.astype(jnp.bfloat16),
            offset.astype(jnp.bfloat16),
            live_row.astype(jnp.bfloat16),
        ],
        axis=1,
    )
    slot_ids = jnp.arange(slot_total, dtype=jnp.int32)
    matches = slot_of[None, :] == slot_ids[:, None]
    filled = jnp.any(matches, axis=1)
    source = jnp.sum(jnp.where(matches, block_ids[None, :], 0), axis=1)
    send = jnp.where(filled[:, None, None], packed[source], jnp.zeros((), jnp.bfloat16))
    got_own = lax.all_to_all(send, "tile", split_axis=0, concat_axis=0, tiled=True)
    got_other = from_partner(got_own, "tile", mirror_bit)
    table = kernel.T.astype(jnp.bfloat16)

    own_flags = slot_flags(got_own, channels, False)
    partial_grid = run_grid(own_flags, table, got_own, channels, False)
    other_flags = slot_flags(got_other, channels, True)
    grid_sum, symmetric = run_grid(other_flags, table, got_other, channels, True, partial_grid)
    combined_grid = lax.psum_scatter(grid_sum, "chan", scatter_dimension=1, tiled=True)
    own_results = run_degrid(own_flags, table, got_own, symmetric)
    returned_slots = lax.all_to_all(own_results, "tile", split_axis=0, concat_axis=0, tiled=True)
    returned = jnp.where(
        is_live[:, None, None, None], returned_slots[slot_of], jnp.zeros((), jnp.bfloat16)
    )
    residual = (visibility.astype(jnp.float32) - returned.astype(jnp.float32)).astype(jnp.bfloat16)
    return (combined_grid, residual)


def solution(mesh):
    placed = (
        P("tile", None, "chan", None),
        P("tile", "chan", None),
        P("tile", None, None),
        P("tile", None),
        P("tile"),
        P("tile"),
        P(),
    )
    return jax.shard_map(
        per_device,
        mesh=mesh,
        in_specs=placed,
        out_specs=(P(None, ("tile", "chan"), None), P("tile", None, "chan", None)),
        check_vma=False,
    )
```
